32 devices in a mesh: groups: 2 (over x), chan: 16 (over z, y, core).
Axes of the slice: x: 2, y: 2, z: 4, core: 2. Of those that a mesh axis runs over, the one named last changes fastest.
Arguments:
- sky_data: bfloat16 [1024, 512, 2, 256], P('groups', 'chan'), parts along dimension 0, may hold values from -1.1953125 to 1.1953125
- beam_gains: bfloat16 [1024, 512, 256], P('groups', 'chan'), parts along dimension 0, may hold values from 0.099609375 to 1
- mixing: float32 [1024, 4], P(('groups', 'chan')), parts along dimension 0, may hold values from -0.25 to 0.25
- noise_levels: int32 [512], P('chan'), may hold values from 1 to 16
- threshold_levels: int32 [4, 2], replicated, may hold values from 1 to 8
- start_sources: float32 [1024, 4, 256], P(('groups', 'chan')), parts along dimension 0, may hold values from -6 to 6
Outputs:
- sources: float32 [1024, 4, 256], P(('groups', 'chan')), parts along dimension 0
The draws below stay inside these ranges and needn't reach their ends.
There are 2 independent parts, one for each index of `groups`. The reference program is written for one: setup_inputs(seed, part) draws one part's arguments, and reference() takes and returns one part's arrays. A program takes and returns all parts, laid end to end along the dimension named above; an argument that names none is the same for every part. Nothing has to cross between parts.
All inputs are finite; a program needn't handle non-finite values.
Results may differ from the reference program's by a relative error of at most 0.025.
Values may be sent and summed in bfloat16 or wider, within the bound.
No kernel may reach another device: no remote copies, remote signals or barrier semaphores. Data moves between devices by JAX's collectives and lax.ppermute only.
A program may use at most 128 MiB of HBM per device.

```python
import math
import jax
import jax.numpy as jnp
from jax import lax

CHANNELS = 512
NROW = 512
NCOL = 256
NS = 4
ITERS = 2
N_CHAN = 16


def set_ends(values, own_key, smallest, high):
    extent = values.shape
    spot = [jax.random.randint(jax.random.fold_in(own_key, axis), (), 0, extent[axis]) for axis in range(len(extent))]
    values = values.at[tuple(spot)].set(smallest)
    longest = extent.index(max(extent))
    spot[longest] = (spot[longest] + 1) % extent[longest]
    return values.at[tuple(spot)].set(high)


def level_of(own_key, shape, shards, low, top_value):
    def one(position, parts):
        draws = jax.random.uniform(jax.random.fold_in(jax.random.fold_in(own_key, 6), position), (parts,), jnp.float32, low / len(shards), top_value / len(shards))
        return jnp.repeat(jnp.exp(draws), shape[position] // parts).reshape((-1,) + (1,) * (len(shape) - position - 1))

    level = one(*shards[0])
    for cut in shards[1:]:
        level = level * one(*cut)
    return level


def bell_draw(rng, dims, scale, most, split=(), kind=jnp.bfloat16):
    drawn = jax.random.normal(rng, dims, jnp.float32) * scale
    if len(split) > 0:
        drawn = level_of(rng, dims, split, -0.22, 0.18) * drawn
    return jnp.clip(drawn, min=-most, max=most).astype(kind)


def setup_inputs(seed: int = 0, part: int = 0) -> dict:
    splits = jax.random.split(jax.random.key(seed), 7)
    part_splits = jax.random.split(jax.random.fold_in(splits[6], part), 7)
    sky_data = bell_draw(part_splits[0], (NROW, CHANNELS, 2, NCOL), 0.2, 1.1953125, ((1, 16),))
    beam_gains = jnp.clip(jnp.exp(math.log(1.0) - 2.306499 * jax.random.uniform(part_splits[1], (NROW, CHANNELS, NCOL), jnp.float32) ** level_of(part_splits[1], (NROW, CHANNELS, NCOL), ((1, 16),), -0.2, 0.2)), 0.099609375, 1.0).astype(jnp.bfloat16)
    mixing = bell_draw(part_splits[2], (CHANNELS, NS), CHANNELS ** -0.5, 0.25, ((0, 16),), jnp.float32)
    noise_levels = set_ends(jax.random.randint(splits[3], (CHANNELS,), 1, 17), jax.random.fold_in(splits[3], 1), 1, 16).astype(jnp.int32)
    threshold_levels = set_ends(jax.random.randint(splits[4], (NS, 2), 1, 9), jax.random.fold_in(splits[4], 1), 1, 8).astype(jnp.int32)
    start_sources = bell_draw(part_splits[5], (NROW, NS, NCOL), 1.0, 6.0, ((0, 16),), jnp.float32)
    return {"sky_data": sky_data, "beam_gains": beam_gains, "mixing": mixing, "noise_levels": noise_levels, "threshold_levels": threshold_levels, "start_sources": start_sources}


def dft_tables(length):
    positions = jnp.arange(length, dtype=jnp.int32)
    angles = (positions[:, None] * positions[None, :] % length).astype(jnp.float32) * (2.0 * math.pi / length)
    norm_factor = 1.0 / math.sqrt(length)
    return ((jnp.cos(angles) * norm_factor).astype(jnp.bfloat16), (-jnp.sin(angles) * norm_factor).astype(jnp.bfloat16))

def column_part(rounded, col_cat):
    row_count, source_count, col_count = rounded.shape
    product = jnp.dot(rounded.reshape(row_count * source_count, col_count), col_cat, preferred_element_type=jnp.float32)
    return product.astype(jnp.bfloat16).reshape(row_count, source_count * 2 * col_count)

def combine_forward(real_prod, imag_prod, source_count, col_count):
    real_prod = real_prod.reshape(real_prod.shape[0], source_count, 2, col_count)
    imag_prod = imag_prod.reshape(imag_prod.shape[0], source_count, 2, col_count)
    real_out = real_prod[:, :, 0] - imag_prod[:, :, 1]
    imag_out = real_prod[:, :, 1] + imag_prod[:, :, 0]
    return jnp.stack([real_out, imag_out], axis=2)

def inverse_rows(row_real, row_imag, packed_grad, col_back, source_count, col_count):
    real_prod = jnp.dot(row_real, packed_grad, preferred_element_type=jnp.float32)
    imag_prod = jnp.dot(row_imag, packed_grad, preferred_element_type=jnp.float32)
    real_prod = real_prod.reshape(real_prod.shape[0], source_count, 2, col_count)
    imag_prod = imag_prod.reshape(imag_prod.shape[0], source_count, 2, col_count)
    real_out = real_prod[:, :, 0] + imag_prod[:, :, 1]
    imag_out = real_prod[:, :, 1] - imag_prod[:, :, 0]
    joined = jnp.concatenate([real_out, imag_out], axis=-1).astype(jnp.bfloat16)
    result = jnp.dot(joined.reshape(-1, 2 * col_count), col_back, preferred_element_type=jnp.float32)
    return result.reshape(real_prod.shape[0], source_count, col_count)

def block_gradient(fourier, data_block, beam_block, mix_block, level_block):
    predicted = jnp.einsum('ct,ktzl->kczl', mix_block.astype(jnp.float32), fourier.astype(jnp.float32))
    beam_gain = beam_block.astype(jnp.float32)[:, :, None, :]
    residual = data_block.astype(jnp.float32) - beam_gain * predicted
    weight = level_block.astype(jnp.float32) * 0.25
    weighted = weight[None, :, None, None] * beam_gain * residual
    summed = jnp.einsum('cs,kczl->kszl', mix_block.astype(jnp.float32), weighted)
    return summed.astype(jnp.bfloat16)

def smooth_cols(values, spacing):
    padded = jnp.pad(values, ((0, 0), (0, 0), (spacing, spacing)))
    return (padded[..., :-2 * spacing] + 2.0 * padded[..., spacing:-spacing] + padded[..., 2 * spacing:]) * 0.25

def smooth_whole(values, spacing):
    padded = jnp.pad(values, ((spacing, spacing), (0, 0), (0, 0)))
    row_done = (padded[:-2 * spacing] + 2.0 * padded[spacing:-spacing] + padded[2 * spacing:]) * 0.25
    return smooth_cols(row_done, spacing)

def shrink(values, bound_value):
    return values - jnp.clip(values, -bound_value, bound_value)

def combine_scales(updated, smooth_one, coarse, fine_bound, coarse_bound):
    return coarse + shrink(smooth_one - coarse, coarse_bound) + shrink(updated - smooth_one, fine_bound)

def reference(sky_data, beam_gains, mixing, noise_levels, threshold_levels, start_sources):
    row_real, row_imag = dft_tables(NROW)
    col_real, col_imag = dft_tables(NCOL)
    col_cat = jnp.concatenate([col_real, col_imag], axis=1)
    col_back = jnp.concatenate([col_real, col_imag], axis=0)
    bounds = threshold_levels.astype(jnp.float32) * 0.05
    fine_bound = bounds[:, 0][:, None]
    coarse_bound = bounds[:, 1][:, None]
    block_size = CHANNELS // N_CHAN
    sources = start_sources
    for iteration in range(ITERS):
        rounded = sources.astype(jnp.bfloat16)
        packed = column_part(rounded, col_cat)
        fourier = combine_forward(jnp.dot(row_real, packed, preferred_element_type=jnp.float32), jnp.dot(row_imag, packed, preferred_element_type=jnp.float32), NS, NCOL)

        def add_block(block_index, running):
            offset = (block_index * block_size).astype(jnp.int32)
            data_block = lax.dynamic_slice_in_dim(sky_data, offset, block_size, 1)
            beam_block = lax.dynamic_slice_in_dim(beam_gains, offset, block_size, 1)
            mix_block = lax.dynamic_slice_in_dim(mixing, offset, block_size, 0)
            level_block = lax.dynamic_slice_in_dim(noise_levels, offset, block_size, 0)
            grad_block = block_gradient(fourier, data_block, beam_block, mix_block, level_block)
            packed_grad = grad_block.reshape(NROW, NS * 2 * NCOL)
            return running + inverse_rows(row_real, row_imag, packed_grad, col_back, NS, NCOL)
        gradient = lax.fori_loop(0, N_CHAN, add_block, jnp.zeros((NROW, NS, NCOL), jnp.float32))
        updated = sources + gradient
        smooth_one = smooth_whole(updated, 1)
        coarse = smooth_whole(smooth_one, 2)
        sources = combine_scales(updated, smooth_one, coarse, fine_bound, coarse_bound)
    return sources
```

```python
import math

import jax
import jax.numpy as jnp
from jax import lax
from jax.sharding import PartitionSpec as P

ITERS = 2


def padded_2(cells, sides, width):
    for axis, dim in sides:
        count = lax.axis_size(axis)
        ends = count - 1
        head = lax.slice_in_dim(cells, 0, width, axis=dim)
        tail = lax.slice_in_dim(cells, cells.shape[dim] - width, cells.shape[dim], axis=dim)
        cells = jnp.concatenate(
            [
                lax.ppermute(tail, axis, [(i, (i + 1) % count) for i in range(ends)]),
                cells,
                lax.ppermute(head, axis, [((i + 1) % count, i) for i in range(ends)]),
            ],
            axis=dim,
        )
    return cells


def gather_rows(strip, axis):
    count = lax.axis_size(axis)
    copies = jnp.broadcast_to(strip[None], (count,) + strip.shape)
    joined = lax.all_to_all(copies, axis, 0, 0, tiled=True)
    return joined.reshape((count * strip.shape[0],) + strip.shape[1:])


def sum_rows(values, axis):
    count = lax.axis_size(axis)
    chunks = values.reshape((count, values.shape[0] // count) + values.shape[1:])
    received = lax.all_to_all(chunks, axis, 0, 0, tiled=True)
    return received.sum(axis=0)


def dft_tables(length):
    positions = jnp.arange(length, dtype=jnp.int32)
    angles = (positions[:, None] * positions[None, :] % length).astype(jnp.float32) * (
        2.0 * math.pi / length
    )
    norm_factor = 1.0 / math.sqrt(length)
    return (
        (jnp.cos(angles) * norm_factor).astype(jnp.bfloat16),
        (-jnp.sin(angles) * norm_factor).astype(jnp.bfloat16),
    )


def column_part(rounded, col_cat):
    row_count, source_count, col_count = rounded.shape
    product = jnp.dot(
        rounded.reshape(row_count * source_count, col_count),
        col_cat,
        preferred_element_type=jnp.float32,
    )
    return product.astype(jnp.bfloat16).reshape(row_count, source_count * 2 * col_count)


def combine_forward(real_prod, imag_prod, source_count, col_count):
    real_prod = real_prod.reshape(real_prod.shape[0], source_count, 2, col_count)
    imag_prod = imag_prod.reshape(imag_prod.shape[0], source_count, 2, col_count)
    real_out = real_prod[:, :, 0] - imag_prod[:, :, 1]
    imag_out = real_prod[:, :, 1] + imag_prod[:, :, 0]
    return jnp.stack([real_out, imag_out], axis=2)


def inverse_rows(row_real, row_imag, packed_grad, col_back, source_count, col_count):
    real_prod = jnp.dot(row_real, packed_grad, preferred_element_type=jnp.float32)
    imag_prod = jnp.dot(row_imag, packed_grad, preferred_element_type=jnp.float32)
    real_prod = real_prod.reshape(real_prod.shape[0], source_count, 2, col_count)
    imag_prod = imag_prod.reshape(imag_prod.shape[0], source_count, 2, col_count)
    real_out = real_prod[:, :, 0] + imag_prod[:, :, 1]
    imag_out = real_prod[:, :, 1] - imag_prod[:, :, 0]
    joined = jnp.concatenate([real_out, imag_out], axis=-1).astype(jnp.bfloat16)
    result = jnp.dot(
        joined.reshape(-1, 2 * col_count), col_back, preferred_element_type=jnp.float32
    )
    return result.reshape(real_prod.shape[0], source_count, col_count)


def block_gradient(fourier, data_block, beam_block, mix_block, level_block):
    predicted = jnp.einsum("ct,ktzl->kczl", mix_block, fourier)
    beam_gain = beam_block.astype(jnp.float32)[:, :, None, :]
    residual = data_block.astype(jnp.float32) - beam_gain * predicted
    weight = level_block.astype(jnp.float32) * 0.25
    weighted = weight[None, :, None, None] * beam_gain * residual
    summed = jnp.einsum("cs,kczl->kszl", mix_block, weighted)
    return summed.astype(jnp.bfloat16)


def smooth_rows(padded, spacing, row_count):
    return (
        padded[0:row_count]
        + 2.0 * padded[spacing : spacing + row_count]
        + padded[2 * spacing : 2 * spacing + row_count]
    ) * 0.25


def smooth_cols(values, spacing):
    padded = jnp.pad(values, ((0, 0), (0, 0), (spacing, spacing)))
    return (
        padded[..., : -2 * spacing]
        + 2.0 * padded[..., spacing:-spacing]
        + padded[..., 2 * spacing :]
    ) * 0.25


def shrink(values, bound_value):
    return values - jnp.clip(values, -bound_value, bound_value)


def combine_scales(updated, smooth_one, coarse, fine_bound, coarse_bound):
    return (
        coarse
        + shrink(smooth_one - coarse, coarse_bound)
        + shrink(updated - smooth_one, fine_bound)
    )


def body(sky_data, beam_gains, mixing, noise_levels, threshold_levels, start_sources):
    strip_rows, source_count, col_count = start_sources.shape
    full_rows = strip_rows * lax.axis_size("chan")
    row_real, row_imag = dft_tables(full_rows)
    col_real, col_imag = dft_tables(col_count)
    col_cat = jnp.concatenate([col_real, col_imag], axis=1)
    col_back = jnp.concatenate([col_real, col_imag], axis=0)
    bounds = threshold_levels.astype(jnp.float32) * 0.05
    fine_bound = bounds[:, 0][:, None]
    coarse_bound = bounds[:, 1][:, None]
    sources = start_sources
    for iteration in range(ITERS):
        rounded = sources.astype(jnp.bfloat16)
        gathered = gather_rows(rounded, "chan")
        packed = column_part(gathered, col_cat)
        fourier = combine_forward(
            jnp.dot(row_real, packed, preferred_element_type=jnp.float32),
            jnp.dot(row_imag, packed, preferred_element_type=jnp.float32),
            source_count,
            col_count,
        )
        grad_local = block_gradient(fourier, sky_data, beam_gains, mixing, noise_levels)
        packed_grad = grad_local.reshape(full_rows, source_count * 2 * col_count)
        gradient = sum_rows(
            inverse_rows(row_real, row_imag, packed_grad, col_back, source_count, col_count),
            "chan",
        )
        updated = sources + gradient
        fine_pad = padded_2(updated, (("chan", 0),), 1)
        smooth_one = smooth_cols(smooth_rows(fine_pad, 1, strip_rows), 1)
        coarse_pad = padded_2(smooth_one, (("chan", 0),), 2)
        coarse = smooth_cols(smooth_rows(coarse_pad, 2, strip_rows), 2)
        sources = combine_scales(updated, smooth_one, coarse, fine_bound, coarse_bound)
    return sources


def solution(mesh):
    return jax.shard_map(
        body,
        mesh=mesh,
        in_specs=(
            P("groups", "chan", None, None),
            P("groups", "chan", None),
            P(("groups", "chan"), None),
            P("chan"),
            P(),
            P(("groups", "chan"), None, None),
        ),
        out_specs=P(("groups", "chan"), None, None),
        check_vma=False,
    )
```

```python
import math

import jax
import jax.numpy as jnp
from jax import lax
from jax.sharding import PartitionSpec as P

ITERS = 2


def padded_2(cells, sides, width):
    for axis, dim in sides:
        count = lax.axis_size(axis)
        ends = count - 1
        head = lax.slice_in_dim(cells, 0, width, axis=dim)
        tail = lax.slice_in_dim(cells, cells.shape[dim] - width, cells.shape[dim], axis=dim)
        cells = jnp.concatenate(
            [
                lax.ppermute(tail, axis, [(i, (i + 1) % count) for i in range(ends)]),
                cells,
                lax.ppermute(head, axis, [((i + 1) % count, i) for i in range(ends)]),
            ],
            axis=dim,
        )
    return cells


def gather_rows(strip, axis):
    count = lax.axis_size(axis)
    bits = count.bit_length() - 1
    assert 1 << bits == count
    own = lax.axis_index(axis)
    joined = strip
    for depth, bit in enumerate(reversed(range(bits))):
        partner = lax.ppermute(joined, axis, [(i, i ^ (1 << bit)) for i in range(count)])
        upper = ((own >> bit) & 1) == 1
        low = jnp.where(upper, partner, joined)
        high = jnp.where(upper, joined, partner)
        joined = jnp.stack([low, high], axis=depth)
    return joined.reshape((count * strip.shape[0],) + strip.shape[1:])


def sum_rows(values, axis):
    count = lax.axis_size(axis)
    bits = count.bit_length() - 1
    assert 1 << bits == count
    own = lax.axis_index(axis)
    split = values.reshape((2,) * bits + (values.shape[0] // count,) + values.shape[1:])
    for bit in range(bits):
        dim = bits - 1 - bit
        side = (own >> bit) & 1
        keep = lax.dynamic_index_in_dim(split, side, axis=dim, keepdims=False)
        send = lax.dynamic_index_in_dim(split, 1 - side, axis=dim, keepdims=False)
        split = keep + lax.ppermute(send, axis, [(i, i ^ (1 << bit)) for i in range(count)])
    return split


def dft_tables(length):
    positions = jnp.arange(length, dtype=jnp.int32)
    angles = (positions[:, None] * positions[None, :] % length).astype(jnp.float32) * (
        2.0 * math.pi / length
    )
    norm_factor = 1.0 / math.sqrt(length)
    return (
        (jnp.cos(angles) * norm_factor).astype(jnp.bfloat16),
        (-jnp.sin(angles) * norm_factor).astype(jnp.bfloat16),
    )


def column_part(rounded, col_cat):
    row_count, source_count, col_count = rounded.shape
    product = jnp.dot(
        rounded.reshape(row_count * source_count, col_count),
        col_cat,
        preferred_element_type=jnp.float32,
    )
    return product.astype(jnp.bfloat16).reshape(row_count, source_count * 2 * col_count)


def combine_forward(real_prod, imag_prod, source_count, col_count):
    real_prod = real_prod.reshape(real_prod.shape[0], source_count, 2, col_count)
    imag_prod = imag_prod.reshape(imag_prod.shape[0], source_count, 2, col_count)
    real_out = real_prod[:, :, 0] - imag_prod[:, :, 1]
    imag_out = real_prod[:, :, 1] + imag_prod[:, :, 0]
    return jnp.stack([real_out, imag_out], axis=2)


def inverse_rows(row_real, row_imag, packed_grad, col_back, source_count, col_count):
    real_prod = jnp.dot(row_real, packed_grad, preferred_element_type=jnp.float32)
    imag_prod = jnp.dot(row_imag, packed_grad, preferred_element_type=jnp.float32)
    real_prod = real_prod.reshape(real_prod.shape[0], source_count, 2, col_count)
    imag_prod = imag_prod.reshape(imag_prod.shape[0], source_count, 2, col_count)
    real_out = real_prod[:, :, 0] + imag_prod[:, :, 1]
    imag_out = real_prod[:, :, 1] - imag_prod[:, :, 0]
    joined = jnp.concatenate([real_out, imag_out], axis=-1).astype(jnp.bfloat16)
    result = jnp.dot(
        joined.reshape(-1, 2 * col_count), col_back, preferred_element_type=jnp.float32
    )
    return result.reshape(real_prod.shape[0], source_count, col_count)


def block_gradient(fourier, data_block, beam_block, mix_block, level_block):
    predicted = jnp.einsum("ct,ktzl->kczl", mix_block, fourier)
    beam_gain = beam_block.astype(jnp.float32)[:, :, None, :]
    residual = data_block.astype(jnp.float32) - beam_gain * predicted
    weight = level_block.astype(jnp.float32) * 0.25
    weighted = weight[None, :, None, None] * beam_gain * residual
    summed = jnp.einsum("cs,kczl->kszl", mix_block, weighted)
    return summed.astype(jnp.bfloat16)


def smooth_rows(padded, spacing, row_count):
    return (
        padded[0:row_count]
        + 2.0 * padded[spacing : spacing + row_count]
        + padded[2 * spacing : 2 * spacing + row_count]
    ) * 0.25


def smooth_cols(values, spacing):
    padded = jnp.pad(values, ((0, 0), (0, 0), (spacing, spacing)))
    return (
        padded[..., : -2 * spacing]
        + 2.0 * padded[..., spacing:-spacing]
        + padded[..., 2 * spacing :]
    ) * 0.25


def shrink(values, bound_value):
    return values - jnp.clip(values, -bound_value, bound_value)


def combine_scales(updated, smooth_one, coarse, fine_bound, coarse_bound):
    return (
        coarse
        + shrink(smooth_one - coarse, coarse_bound)
        + shrink(updated - smooth_one, fine_bound)
    )


def body(sky_data, beam_gains, mixing, noise_levels, threshold_levels, start_sources):
    strip_rows, source_count, col_count = start_sources.shape
    full_rows = strip_rows * lax.axis_size("chan")
    row_real, row_imag = dft_tables(full_rows)
    col_real, col_imag = dft_tables(col_count)
    col_cat = jnp.concatenate([col_real, col_imag], axis=1)
    col_back = jnp.concatenate([col_real, col_imag], axis=0)
    bounds = threshold_levels.astype(jnp.float32) * 0.05
    fine_bound = bounds[:, 0][:, None]
    coarse_bound = bounds[:, 1][:, None]
    sources = start_sources
    for iteration in range(ITERS):
        rounded = sources.astype(jnp.bfloat16)
        gathered = gather_rows(rounded, "chan")
        packed = column_part(gathered, col_cat)
        fourier = combine_forward(
            jnp.dot(row_real, packed, preferred_element_type=jnp.float32),
            jnp.dot(row_imag, packed, preferred_element_type=jnp.float32),
            source_count,
            col_count,
        )
        grad_local = block_gradient(fourier, sky_data, beam_gains, mixing, noise_levels)
        packed_grad = grad_local.reshape(full_rows, source_count * 2 * col_count)
        gradient = sum_rows(
            inverse_rows(row_real, row_imag, packed_grad, col_back, source_count, col_count),
            "chan",
        )
        updated = sources + gradient
        fine_pad = padded_2(updated, (("chan", 0),), 1)
        smooth_one = smooth_cols(smooth_rows(fine_pad, 1, strip_rows), 1)
        coarse_pad = padded_2(smooth_one, (("chan", 0),), 2)
        coarse = smooth_cols(smooth_rows(coarse_pad, 2, strip_rows), 2)
        sources = combine_scales(updated, smooth_one, coarse, fine_bound, coarse_bound)
    return sources


def solution(mesh):
    return jax.shard_map(
        body,
        mesh=mesh,
        in_specs=(
            P("groups", "chan", None, None),
            P("groups", "chan", None),
            P(("groups", "chan"), None),
            P("chan"),
            P(),
            P(("groups", "chan"), None, None),
        ),
        out_specs=P(("groups", "chan"), None, None),
        check_vma=False,
    )
```

```python
import math

import jax
import jax.numpy as jnp
from jax import lax
from jax.sharding import PartitionSpec as P

ITERS = 2


def padded_2(cells, sides, width):
    for axis, dim in sides:
        count = lax.axis_size(axis)
        ends = count - 1
        head = lax.slice_in_dim(cells, 0, width, axis=dim)
        tail = lax.slice_in_dim(cells, cells.shape[dim] - width, cells.shape[dim], axis=dim)
        cells = jnp.concatenate(
            [
                lax.ppermute(tail, axis, [(i, (i + 1) % count) for i in range(ends)]),
                cells,
                lax.ppermute(head, axis, [((i + 1) % count, i) for i in range(ends)]),
            ],
            axis=dim,
        )
    return cells


def gather_rows(strip, axis):
    count = lax.axis_size(axis)
    bits = count.bit_length() - 1
    assert 1 << bits == count
    own = lax.axis_index(axis)
    joined = strip
    for depth, bit in enumerate(reversed(range(bits))):
        partner = lax.ppermute(joined, axis, [(i, i ^ (1 << bit)) for i in range(count)])
        upper = ((own >> bit) & 1) == 1
        low = jnp.where(upper, partner, joined)
        high = jnp.where(upper, joined, partner)
        joined = jnp.stack([low, high], axis=depth)
    return joined.reshape((count * strip.shape[0],) + strip.shape[1:])


def sum_rows(values, axis):
    count = lax.axis_size(axis)
    bits = count.bit_length() - 1
    assert 1 << bits == count
    own = lax.axis_index(axis)
    split = values.reshape((2,) * bits + (values.shape[0] // count,) + values.shape[1:])
    for bit in range(bits):
        dim = bits - 1 - bit
        side = (own >> bit) & 1
        keep = lax.dynamic_index_in_dim(split, side, axis=dim, keepdims=False)
        send = lax.dynamic_index_in_dim(split, 1 - side, axis=dim, keepdims=False)
        split = keep + lax.ppermute(send, axis, [(i, i ^ (1 << bit)) for i in range(count)])
    return split


def dft_tables(length):
    positions = jnp.arange(length, dtype=jnp.int32)
    angles = (positions[:, None] * positions[None, :] % length).astype(jnp.float32) * (
        2.0 * math.pi / length
    )
    norm_factor = 1.0 / math.sqrt(length)
    return (
        (jnp.cos(angles) * norm_factor).astype(jnp.bfloat16),
        (-jnp.sin(angles) * norm_factor).astype(jnp.bfloat16),
    )


def column_part(rounded, col_cat):
    row_count, source_count, col_count = rounded.shape
    product = jnp.dot(
        rounded.reshape(row_count * source_count, col_count),
        col_cat,
        preferred_element_type=jnp.float32,
    )
    return product.astype(jnp.bfloat16).reshape(row_count, source_count * 2 * col_count)


def combine_forward(real_prod, imag_prod, source_count, col_count):
    real_prod = real_prod.reshape(real_prod.shape[0], source_count, 2, col_count)
    imag_prod = imag_prod.reshape(imag_prod.shape[0], source_count, 2, col_count)
    real_out = real_prod[:, :, 0] - imag_prod[:, :, 1]
    imag_out = real_prod[:, :, 1] + imag_prod[:, :, 0]
    return jnp.stack([real_out, imag_out], axis=2)


def inverse_rows(row_real, row_imag, packed_grad, col_back, source_count, col_count):
    real_prod = jnp.dot(row_real, packed_grad, preferred_element_type=jnp.float32)
    imag_prod = jnp.dot(row_imag, packed_grad, preferred_element_type=jnp.float32)
    real_prod = real_prod.reshape(real_prod.shape[0], source_count, 2, col_count)
    imag_prod = imag_prod.reshape(imag_prod.shape[0], source_count, 2, col_count)
    real_out = real_prod[:, :, 0] + imag_prod[:, :, 1]
    imag_out = real_prod[:, :, 1] - imag_prod[:, :, 0]
    joined = jnp.concatenate([real_out, imag_out], axis=-1).astype(jnp.bfloat16)
    result = jnp.dot(
        joined.reshape(-1, 2 * col_count), col_back, preferred_element_type=jnp.float32
    )
    return result.reshape(real_prod.shape[0], source_count, col_count)


def channel_terms(data_block, beam_block, mix_block, level_block):
    beam_gain = beam_block.astype(jnp.float32)
    weight = level_block.astype(jnp.float32) * 0.25
    weighted_mix = mix_block * weight[:, None]
    data_term = jnp.einsum(
        "cs,kczl->kszl",
        weighted_mix,
        data_block.astype(jnp.float32) * beam_gain[:, :, None, :],
        precision=lax.Precision.HIGHEST,
    )
    pair_mix = weighted_mix[:, :, None] * mix_block[:, None, :]
    gain_term = jnp.einsum(
        "cst,kcl->kstl", pair_mix, beam_gain * beam_gain, precision=lax.Precision.HIGHEST
    )
    return data_term, gain_term


def block_gradient(fourier, data_term, gain_term):
    predicted = (gain_term[:, :, :, None, :] * fourier[:, None, :, :, :]).sum(axis=2)
    return (data_term - predicted).astype(jnp.bfloat16)


def smooth_rows(padded, spacing, row_count):
    return (
        padded[0:row_count]
        + 2.0 * padded[spacing : spacing + row_count]
        + padded[2 * spacing : 2 * spacing + row_count]
    ) * 0.25


def smooth_cols(values, spacing):
    padded = jnp.pad(values, ((0, 0), (0, 0), (spacing, spacing)))
    return (
        padded[..., : -2 * spacing]
        + 2.0 * padded[..., spacing:-spacing]
        + padded[..., 2 * spacing :]
    ) * 0.25


def shrink(values, bound_value):
    return values - jnp.clip(values, -bound_value, bound_value)


def combine_scales(updated, smooth_one, coarse, fine_bound, coarse_bound):
    return (
        coarse
        + shrink(smooth_one - coarse, coarse_bound)
        + shrink(updated - smooth_one, fine_bound)
    )


def body(sky_data, beam_gains, mixing, noise_levels, threshold_levels, start_sources):
    strip_rows, source_count, col_count = start_sources.shape
    full_rows = strip_rows * lax.axis_size("chan")
    row_real, row_imag = dft_tables(full_rows)
    col_real, col_imag = dft_tables(col_count)
    col_cat = jnp.concatenate([col_real, col_imag], axis=1)
    col_back = jnp.concatenate([col_real, col_imag], axis=0)
    bounds = threshold_levels.astype(jnp.float32) * 0.05
    fine_bound = bounds[:, 0][:, None]
    coarse_bound = bounds[:, 1][:, None]
    data_term, gain_term = channel_terms(sky_data, beam_gains, mixing, noise_levels)
    sources = start_sources
    for iteration in range(ITERS):
        rounded = sources.astype(jnp.bfloat16)
        gathered = gather_rows(rounded, "chan")
        packed = column_part(gathered, col_cat)
        fourier = combine_forward(
            jnp.dot(row_real, packed, preferred_element_type=jnp.float32),
            jnp.dot(row_imag, packed, preferred_element_type=jnp.float32),
            source_count,
            col_count,
        )
        grad_local = block_gradient(fourier, data_term, gain_term)
        packed_grad = grad_local.reshape(full_rows, source_count * 2 * col_count)
        gradient = sum_rows(
            inverse_rows(row_real, row_imag, packed_grad, col_back, source_count, col_count),
            "chan",
        )
        updated = sources + gradient
        fine_pad = padded_2(updated, (("chan", 0),), 1)
        smooth_one = smooth_cols(smooth_rows(fine_pad, 1, strip_rows), 1)
        coarse_pad = padded_2(smooth_one, (("chan", 0),), 2)
        coarse = smooth_cols(smooth_rows(coarse_pad, 2, strip_rows), 2)
        sources = combine_scales(updated, smooth_one, coarse, fine_bound, coarse_bound)
    return sources


def solution(mesh):
    return jax.shard_map(
        body,
        mesh=mesh,
        in_specs=(
            P("groups", "chan", None, None),
            P("groups", "chan", None),
            P(("groups", "chan"), None),
            P("chan"),
            P(),
            P(("groups", "chan"), None, None),
        ),
        out_specs=P(("groups", "chan"), None, None),
        check_vma=False,
    )
```

```python
import math

import jax
import jax.numpy as jnp
from jax import lax
from jax.sharding import PartitionSpec as P

ITERS = 2


def padded_2(cells, sides, width):
    for axis, dim in sides:
        count = lax.axis_size(axis)
        ends = count - 1
        head = lax.slice_in_dim(cells, 0, width, axis=dim)
        tail = lax.slice_in_dim(cells, cells.shape[dim] - width, cells.shape[dim], axis=dim)
        cells = jnp.concatenate(
            [
                lax.ppermute(tail, axis, [(i, (i + 1) % count) for i in range(ends)]),
                cells,
                lax.ppermute(head, axis, [((i + 1) % count, i) for i in range(ends)]),
            ],
            axis=dim,
        )
    return cells


def gather_rows(strip, axis):
    count = lax.axis_size(axis)
    bits = count.bit_length() - 1
    assert 1 << bits == count
    own = lax.axis_index(axis)
    joined = strip
    for depth, bit in enumerate(reversed(range(bits))):
        partner = lax.ppermute(joined, axis, [(i, i ^ (1 << bit)) for i in range(count)])
        upper = ((own >> bit) & 1) == 1
        low = jnp.where(upper, partner, joined)
        high = jnp.where(upper, joined, partner)
        joined = jnp.stack([low, high], axis=depth)
    return joined.reshape((count * strip.shape[0],) + strip.shape[1:])


def sum_rows(values, axis):
    count = lax.axis_size(axis)
    bits = count.bit_length() - 1
    assert 1 << bits == count
    own = lax.axis_index(axis)
    split = values.reshape((2,) * bits + (values.shape[0] // count,) + values.shape[1:])
    for bit in range(bits):
        dim = bits - 1 - bit
        side = (own >> bit) & 1
        keep = lax.dynamic_index_in_dim(split, side, axis=dim, keepdims=False)
        send = lax.dynamic_index_in_dim(split, 1 - side, axis=dim, keepdims=False)
        moved = lax.ppermute(
            send.astype(jnp.bfloat16), axis, [(i, i ^ (1 << bit)) for i in range(count)]
        )
        split = keep + moved.astype(jnp.float32)
    return split


def dft_tables(length):
    positions = jnp.arange(length, dtype=jnp.int32)
    angles = (positions[:, None] * positions[None, :] % length).astype(jnp.float32) * (
        2.0 * math.pi / length
    )
    norm_factor = 1.0 / math.sqrt(length)
    return (
        (jnp.cos(angles) * norm_factor).astype(jnp.bfloat16),
        (-jnp.sin(angles) * norm_factor).astype(jnp.bfloat16),
    )


def column_part(rounded, col_cat):
    row_count, source_count, col_count = rounded.shape
    product = jnp.dot(
        rounded.reshape(row_count * source_count, col_count),
        col_cat,
        preferred_element_type=jnp.float32,
    )
    return product.astype(jnp.bfloat16).reshape(row_count, source_count * 2 * col_count)


def combine_forward(real_prod, imag_prod, source_count, col_count):
    real_prod = real_prod.reshape(real_prod.shape[0], source_count, 2, col_count)
    imag_prod = imag_prod.reshape(imag_prod.shape[0], source_count, 2, col_count)
    real_out = real_prod[:, :, 0] - imag_prod[:, :, 1]
    imag_out = real_prod[:, :, 1] + imag_prod[:, :, 0]
    return jnp.stack([real_out, imag_out], axis=2)


def inverse_rows(row_real, row_imag, packed_grad, col_back, source_count, col_count):
    real_prod = jnp.dot(row_real, packed_grad, preferred_element_type=jnp.float32)
    imag_prod = jnp.dot(row_imag, packed_grad, preferred_element_type=jnp.float32)
    real_prod = real_prod.reshape(real_prod.shape[0], source_count, 2, col_count)
    imag_prod = imag_prod.reshape(imag_prod.shape[0], source_count, 2, col_count)
    real_out = real_prod[:, :, 0] + imag_prod[:, :, 1]
    imag_out = real_prod[:, :, 1] - imag_prod[:, :, 0]
    joined = jnp.concatenate([real_out, imag_out], axis=-1).astype(jnp.bfloat16)
    result = jnp.dot(
        joined.reshape(-1, 2 * col_count), col_back, preferred_element_type=jnp.float32
    )
    return result.reshape(real_prod.shape[0], source_count, col_count)


def block_diagonal(small, copies):
    rows, cols = small.shape
    eye = jnp.eye(copies, dtype=small.dtype)
    return (eye[:, None, :, None] * small[None, :, None, :]).reshape(copies * rows, copies * cols)


def channel_terms(data_block, beam_block, mix_block, level_block, rows_per_block=8):
    row_count, chan_count, _, col_count = data_block.shape
    source_count = mix_block.shape[1]
    blocks = row_count // rows_per_block
    beam_gain = beam_block.astype(jnp.float32)
    weight = level_block.astype(jnp.float32) * 0.25
    weighted_mix = mix_block * weight[:, None]
    pair_mix = (weighted_mix[:, :, None] * mix_block[:, None, :]).reshape(chan_count, -1)
    beamed = data_block.astype(jnp.float32) * beam_gain[:, :, None, :]
    data_term = jnp.einsum(
        "ij,bjn->bin",
        block_diagonal(weighted_mix.T, rows_per_block),
        beamed.reshape(blocks, rows_per_block * chan_count, 2 * col_count),
        precision=lax.Precision.HIGHEST,
    ).reshape(row_count, source_count, 2, col_count)
    gain_term = jnp.einsum(
        "ij,bjn->bin",
        block_diagonal(pair_mix.T, rows_per_block),
        (beam_gain * beam_gain).reshape(blocks, rows_per_block * chan_count, col_count),
        precision=lax.Precision.HIGHEST,
    ).reshape(row_count, source_count, source_count, col_count)
    return data_term, gain_term


def block_gradient(fourier, data_term, gain_term):
    predicted = (gain_term[:, :, :, None, :] * fourier[:, None, :, :, :]).sum(axis=2)
    return (data_term - predicted).astype(jnp.bfloat16)


def smooth_rows(padded, spacing, row_count):
    return (
        padded[0:row_count]
        + 2.0 * padded[spacing : spacing + row_count]
        + padded[2 * spacing : 2 * spacing + row_count]
    ) * 0.25


def smooth_cols(values, spacing):
    padded = jnp.pad(values, ((0, 0), (0, 0), (spacing, spacing)))
    return (
        padded[..., : -2 * spacing]
        + 2.0 * padded[..., spacing:-spacing]
        + padded[..., 2 * spacing :]
    ) * 0.25


def shrink(values, bound_value):
    return values - jnp.clip(values, -bound_value, bound_value)


def combine_scales(updated, smooth_one, coarse, fine_bound, coarse_bound):
    return (
        coarse
        + shrink(smooth_one - coarse, coarse_bound)
        + shrink(updated - smooth_one, fine_bound)
    )


def body(sky_data, beam_gains, mixing, noise_levels, threshold_levels, start_sources):
    strip_rows, source_count, col_count = start_sources.shape
    full_rows = strip_rows * lax.axis_size("chan")
    row_real, row_imag = dft_tables(full_rows)
    col_real, col_imag = dft_tables(col_count)
    col_cat = jnp.concatenate([col_real, col_imag], axis=1)
    col_back = jnp.concatenate([col_real, col_imag], axis=0)
    bounds = threshold_levels.astype(jnp.float32) * 0.05
    fine_bound = bounds[:, 0][:, None]
    coarse_bound = bounds[:, 1][:, None]
    data_term, gain_term = channel_terms(sky_data, beam_gains, mixing, noise_levels)
    sources = start_sources
    for iteration in range(ITERS):
        rounded = sources.astype(jnp.bfloat16)
        gathered = gather_rows(rounded, "chan")
        packed = column_part(gathered, col_cat)
        fourier = combine_forward(
            jnp.dot(row_real, packed, preferred_element_type=jnp.float32),
            jnp.dot(row_imag, packed, preferred_element_type=jnp.float32),
            source_count,
            col_count,
        )
        grad_local = block_gradient(fourier, data_term, gain_term)
        packed_grad = grad_local.reshape(full_rows, source_count * 2 * col_count)
        gradient = sum_rows(
            inverse_rows(row_real, row_imag, packed_grad, col_back, source_count, col_count),
            "chan",
        )
        updated = sources + gradient
        fine_pad = padded_2(updated, (("chan", 0),), 1)
        smooth_one = smooth_cols(smooth_rows(fine_pad, 1, strip_rows), 1)
        coarse_pad = padded_2(smooth_one, (("chan", 0),), 2)
        coarse = smooth_cols(smooth_rows(coarse_pad, 2, strip_rows), 2)
        sources = combine_scales(updated, smooth_one, coarse, fine_bound, coarse_bound)
    return sources


def solution(mesh):
    return jax.shard_map(
        body,
        mesh=mesh,
        in_specs=(
            P("groups", "chan", None, None),
            P("groups", "chan", None),
            P(("groups", "chan"), None),
            P("chan"),
            P(),
            P(("groups", "chan"), None, None),
        ),
        out_specs=P(("groups", "chan"), None, None),
        check_vma=False,
    )
```

```python
import math

import jax
import jax.numpy as jnp
from jax import lax
from jax.sharding import PartitionSpec as P

ITERS = 2


def padded_2(cells, sides, width):
    for axis, dim in sides:
        count = lax.axis_size(axis)
        ends = count - 1
        head = lax.slice_in_dim(cells, 0, width, axis=dim)
        tail = lax.slice_in_dim(cells, cells.shape[dim] - width, cells.shape[dim], axis=dim)
        cells = jnp.concatenate(
            [
                lax.ppermute(tail, axis, [(i, (i + 1) % count) for i in range(ends)]),
                cells,
                lax.ppermute(head, axis, [((i + 1) % count, i) for i in range(ends)]),
            ],
            axis=dim,
        )
    return cells


def gather_rows(strip, axis):
    count = lax.axis_size(axis)
    copies = jnp.broadcast_to(strip[None], (count,) + strip.shape)
    joined = lax.all_to_all(copies, axis, 0, 0, tiled=True)
    return joined.reshape((count * strip.shape[0],) + strip.shape[1:])


def sum_rows(values, axis):
    count = lax.axis_size(axis)
    chunks = values.reshape((count, values.shape[0] // count) + values.shape[1:])
    received = lax.all_to_all(chunks.astype(jnp.bfloat16), axis, 0, 0, tiled=True)
    return received.astype(jnp.float32).sum(axis=0)


def dft_tables(length):
    positions = jnp.arange(length, dtype=jnp.int32)
    angles = (positions[:, None] * positions[None, :] % length).astype(jnp.float32) * (
        2.0 * math.pi / length
    )
    norm_factor = 1.0 / math.sqrt(length)
    return (
        (jnp.cos(angles) * norm_factor).astype(jnp.bfloat16),
        (-jnp.sin(angles) * norm_factor).astype(jnp.bfloat16),
    )


def column_part(rounded, col_cat):
    row_count, source_count, col_count = rounded.shape
    product = jnp.dot(
        rounded.reshape(row_count * source_count, col_count),
        col_cat,
        preferred_element_type=jnp.float32,
    )
    return product.astype(jnp.bfloat16).reshape(row_count, source_count * 2 * col_count)


def combine_forward(real_prod, imag_prod, source_count, col_count):
    real_prod = real_prod.reshape(real_prod.shape[0], source_count, 2, col_count)
    imag_prod = imag_prod.reshape(imag_prod.shape[0], source_count, 2, col_count)
    real_out = real_prod[:, :, 0] - imag_prod[:, :, 1]
    imag_out = real_prod[:, :, 1] + imag_prod[:, :, 0]
    return jnp.stack([real_out, imag_out], axis=2)


def inverse_rows(row_real, row_imag, packed_grad, col_back, source_count, col_count):
    real_prod = jnp.dot(row_real, packed_grad, preferred_element_type=jnp.float32)
    imag_prod = jnp.dot(row_imag, packed_grad, preferred_element_type=jnp.float32)
    real_prod = real_prod.reshape(real_prod.shape[0], source_count, 2, col_count)
    imag_prod = imag_prod.reshape(imag_prod.shape[0], source_count, 2, col_count)
    real_out = real_prod[:, :, 0] + imag_prod[:, :, 1]
    imag_out = real_prod[:, :, 1] - imag_prod[:, :, 0]
    joined = jnp.concatenate([real_out, imag_out], axis=-1).astype(jnp.bfloat16)
    result = jnp.dot(
        joined.reshape(-1, 2 * col_count), col_back, preferred_element_type=jnp.float32
    )
    return result.reshape(real_prod.shape[0], source_count, col_count)


def block_gradient(fourier, data_block, beam_block, mix_block, level_block):
    predicted = jnp.einsum("ct,ktzl->kczl", mix_block, fourier)
    beam_gain = beam_block.astype(jnp.float32)[:, :, None, :]
    residual = data_block.astype(jnp.float32) - beam_gain * predicted
    weight = level_block.astype(jnp.float32) * 0.25
    weighted = weight[None, :, None, None] * beam_gain * residual
    summed = jnp.einsum("cs,kczl->kszl", mix_block, weighted)
    return summed.astype(jnp.bfloat16)


def smooth_rows(padded, spacing, row_count):
    return (
        padded[0:row_count]
        + 2.0 * padded[spacing : spacing + row_count]
        + padded[2 * spacing : 2 * spacing + row_count]
    ) * 0.25


def smooth_cols(values, spacing):
    padded = jnp.pad(values, ((0, 0), (0, 0), (spacing, spacing)))
    return (
        padded[..., : -2 * spacing]
        + 2.0 * padded[..., spacing:-spacing]
        + padded[..., 2 * spacing :]
    ) * 0.25


def shrink(values, bound_value):
    return values - jnp.clip(values, -bound_value, bound_value)


def combine_scales(updated, smooth_one, coarse, fine_bound, coarse_bound):
    return (
        coarse
        + shrink(smooth_one - coarse, coarse_bound)
        + shrink(updated - smooth_one, fine_bound)
    )


def body(sky_data, beam_gains, mixing, noise_levels, threshold_levels, start_sources):
    strip_rows, source_count, col_count = start_sources.shape
    full_rows = strip_rows * lax.axis_size("chan")
    row_real, row_imag = dft_tables(full_rows)
    col_real, col_imag = dft_tables(col_count)
    col_cat = jnp.concatenate([col_real, col_imag], axis=1)
    col_back = jnp.concatenate([col_real, col_imag], axis=0)
    bounds = threshold_levels.astype(jnp.float32) * 0.05
    fine_bound = bounds[:, 0][:, None]
    coarse_bound = bounds[:, 1][:, None]
    sources = start_sources
    for iteration in range(ITERS):
        rounded = sources.astype(jnp.bfloat16)
        gathered = gather_rows(rounded, "chan")
        packed = column_part(gathered, col_cat)
        fourier = combine_forward(
            jnp.dot(row_real, packed, preferred_element_type=jnp.float32),
            jnp.dot(row_imag, packed, preferred_element_type=jnp.float32),
            source_count,
            col_count,
        )
        grad_local = block_gradient(fourier, sky_data, beam_gains, mixing, noise_levels)
        packed_grad = grad_local.reshape(full_rows, source_count * 2 * col_count)
        gradient = sum_rows(
            inverse_rows(row_real, row_imag, packed_grad, col_back, source_count, col_count),
            "chan",
        )
        updated = sources + gradient
        fine_pad = padded_2(updated, (("chan", 0),), 1)
        smooth_one = smooth_cols(smooth_rows(fine_pad, 1, strip_rows), 1)
        coarse_pad = padded_2(smooth_one, (("chan", 0),), 2)
        coarse = smooth_cols(smooth_rows(coarse_pad, 2, strip_rows), 2)
        sources = combine_scales(updated, smooth_one, coarse, fine_bound, coarse_bound)
    return sources


def solution(mesh):
    return jax.shard_map(
        body,
        mesh=mesh,
        in_specs=(
            P("groups", "chan", None, None),
            P("groups", "chan", None),
            P(("groups", "chan"), None),
            P("chan"),
            P(),
            P(("groups", "chan"), None, None),
        ),
        out_specs=P(("groups", "chan"), None, None),
        check_vma=False,
    )
```

```python
import math

import jax
import jax.numpy as jnp
from jax import lax
from jax.sharding import PartitionSpec as P

ITERS = 2


def padded_2(cells, sides, width):
    for axis, dim in sides:
        count = lax.axis_size(axis)
        ends = count - 1
        head = lax.slice_in_dim(cells, 0, width, axis=dim)
        tail = lax.slice_in_dim(cells, cells.shape[dim] - width, cells.shape[dim], axis=dim)
        cells = jnp.concatenate(
            [
                lax.ppermute(tail, axis, [(i, (i + 1) % count) for i in range(ends)]),
                cells,
                lax.ppermute(head, axis, [((i + 1) % count, i) for i in range(ends)]),
            ],
            axis=dim,
        )
    return cells


def gather_rows(strip, axis):
    count = lax.axis_size(axis)
    bits = count.bit_length() - 1
    assert 1 << bits == count
    own = lax.axis_index(axis)
    joined = strip
    for depth, bit in enumerate(reversed(range(bits))):
        partner = lax.ppermute(joined, axis, [(i, i ^ (1 << bit)) for i in range(count)])
        upper = ((own >> bit) & 1) == 1
        low = jnp.where(upper, partner, joined)
        high = jnp.where(upper, joined, partner)
        joined = jnp.stack([low, high], axis=depth)
    return joined.reshape((count * strip.shape[0],) + strip.shape[1:])


def sum_rows(values, axis):
    count = lax.axis_size(axis)
    chunks = values.reshape((count, values.shape[0] // count) + values.shape[1:])
    received = lax.all_to_all(chunks.astype(jnp.bfloat16), axis, 0, 0, tiled=True)
    return received.astype(jnp.float32).sum(axis=0)


def dft_tables(length):
    positions = jnp.arange(length, dtype=jnp.int32)
    angles = (positions[:, None] * positions[None, :] % length).astype(jnp.float32) * (
        2.0 * math.pi / length
    )
    norm_factor = 1.0 / math.sqrt(length)
    return (
        (jnp.cos(angles) * norm_factor).astype(jnp.bfloat16),
        (-jnp.sin(angles) * norm_factor).astype(jnp.bfloat16),
    )


def column_part(rounded, col_cat):
    row_count, source_count, col_count = rounded.shape
    product = jnp.dot(
        rounded.reshape(row_count * source_count, col_count),
        col_cat,
        preferred_element_type=jnp.float32,
    )
    return product.astype(jnp.bfloat16).reshape(row_count, source_count * 2 * col_count)


def combine_forward(real_prod, imag_prod, source_count, col_count):
    real_prod = real_prod.reshape(real_prod.shape[0], source_count, 2, col_count)
    imag_prod = imag_prod.reshape(imag_prod.shape[0], source_count, 2, col_count)
    real_out = real_prod[:, :, 0] - imag_prod[:, :, 1]
    imag_out = real_prod[:, :, 1] + imag_prod[:, :, 0]
    return jnp.stack([real_out, imag_out], axis=2)


def inverse_rows(row_real, row_imag, packed_grad, col_back, source_count, col_count):
    real_prod = jnp.dot(row_real, packed_grad, preferred_element_type=jnp.float32)
    imag_prod = jnp.dot(row_imag, packed_grad, preferred_element_type=jnp.float32)
    real_prod = real_prod.reshape(real_prod.shape[0], source_count, 2, col_count)
    imag_prod = imag_prod.reshape(imag_prod.shape[0], source_count, 2, col_count)
    real_out = real_prod[:, :, 0] + imag_prod[:, :, 1]
    imag_out = real_prod[:, :, 1] - imag_prod[:, :, 0]
    joined = jnp.concatenate([real_out, imag_out], axis=-1).astype(jnp.bfloat16)
    result = jnp.dot(
        joined.reshape(-1, 2 * col_count), col_back, preferred_element_type=jnp.float32
    )
    return result.reshape(real_prod.shape[0], source_count, col_count)


def block_gradient(fourier, data_block, beam_block, mix_block, level_block):
    predicted = jnp.einsum("ct,ktzl->kczl", mix_block, fourier)
    beam_gain = beam_block.astype(jnp.float32)[:, :, None, :]
    residual = data_block.astype(jnp.float32) - beam_gain * predicted
    weight = level_block.astype(jnp.float32) * 0.25
    weighted = weight[None, :, None, None] * beam_gain * residual
    summed = jnp.einsum("cs,kczl->kszl", mix_block, weighted)
    return summed.astype(jnp.bfloat16)


def smooth_rows(padded, spacing, row_count):
    return (
        padded[0:row_count]
        + 2.0 * padded[spacing : spacing + row_count]
        + padded[2 * spacing : 2 * spacing + row_count]
    ) * 0.25


def smooth_cols(values, spacing):
    padded = jnp.pad(values, ((0, 0), (0, 0), (spacing, spacing)))
    return (
        padded[..., : -2 * spacing]
        + 2.0 * padded[..., spacing:-spacing]
        + padded[..., 2 * spacing :]
    ) * 0.25


def shrink(values, bound_value):
    return values - jnp.clip(values, -bound_value, bound_value)


def combine_scales(updated, smooth_one, coarse, fine_bound, coarse_bound):
    return (
        coarse
        + shrink(smooth_one - coarse, coarse_bound)
        + shrink(updated - smooth_one, fine_bound)
    )


def body(sky_data, beam_gains, mixing, noise_levels, threshold_levels, start_sources):
    strip_rows, source_count, col_count = start_sources.shape
    full_rows = strip_rows * lax.axis_size("chan")
    row_real, row_imag = dft_tables(full_rows)
    col_real, col_imag = dft_tables(col_count)
    col_cat = jnp.concatenate([col_real, col_imag], axis=1)
    col_back = jnp.concatenate([col_real, col_imag], axis=0)
    bounds = threshold_levels.astype(jnp.float32) * 0.05
    fine_bound = bounds[:, 0][:, None]
    coarse_bound = bounds[:, 1][:, None]
    sources = start_sources
    for iteration in range(ITERS):
        rounded = sources.astype(jnp.bfloat16)
        gathered = gather_rows(rounded, "chan")
        packed = column_part(gathered, col_cat)
        fourier = combine_forward(
            jnp.dot(row_real, packed, preferred_element_type=jnp.float32),
            jnp.dot(row_imag, packed, preferred_element_type=jnp.float32),
            source_count,
            col_count,
        )
        grad_local = block_gradient(fourier, sky_data, beam_gains, mixing, noise_levels)
        packed_grad = grad_local.reshape(full_rows, source_count * 2 * col_count)
        gradient = sum_rows(
            inverse_rows(row_real, row_imag, packed_grad, col_back, source_count, col_count),
            "chan",
        )
        updated = sources + gradient
        fine_pad = padded_2(updated, (("chan", 0),), 1)
        smooth_one = smooth_cols(smooth_rows(fine_pad, 1, strip_rows), 1)
        coarse_pad = padded_2(smooth_one, (("chan", 0),), 2)
        coarse = smooth_cols(smooth_rows(coarse_pad, 2, strip_rows), 2)
        sources = combine_scales(updated, smooth_one, coarse, fine_bound, coarse_bound)
    return sources


def solution(mesh):
    return jax.shard_map(
        body,
        mesh=mesh,
        in_specs=(
            P("groups", "chan", None, None),
            P("groups", "chan", None),
            P(("groups", "chan"), None),
            P("chan"),
            P(),
            P(("groups", "chan"), None, None),
        ),
        out_specs=P(("groups", "chan"), None, None),
        check_vma=False,
    )
```

```python
import math

import jax
import jax.numpy as jnp
from jax import lax
from jax.sharding import PartitionSpec as P

ITERS = 2


def padded_2(cells, sides, width):
    for axis, dim in sides:
        count = lax.axis_size(axis)
        ends = count - 1
        head = lax.slice_in_dim(cells, 0, width, axis=dim)
        tail = lax.slice_in_dim(cells, cells.shape[dim] - width, cells.shape[dim], axis=dim)
        cells = jnp.concatenate(
            [
                lax.ppermute(tail, axis, [(i, (i + 1) % count) for i in range(ends)]),
                cells,
                lax.ppermute(head, axis, [((i + 1) % count, i) for i in range(ends)]),
            ],
            axis=dim,
        )
    return cells


def gather_all(strip, axis):
    count = lax.axis_size(axis)
    copies = jnp.broadcast_to(strip[None], (count,) + strip.shape)
    joined = lax.all_to_all(copies, axis, 0, 0, tiled=True)
    return joined.reshape((count * strip.shape[0],) + strip.shape[1:])


def gather_rows(strip, axis):
    count = lax.axis_size(axis)
    bits = count.bit_length() - 1
    assert 1 << bits == count
    own = lax.axis_index(axis)
    joined = strip
    for depth, bit in enumerate(reversed(range(bits))):
        partner = lax.ppermute(joined, axis, [(i, i ^ (1 << bit)) for i in range(count)])
        upper = ((own >> bit) & 1) == 1
        low = jnp.where(upper, partner, joined)
        high = jnp.where(upper, joined, partner)
        joined = jnp.stack([low, high], axis=depth)
    return joined.reshape((count * strip.shape[0],) + strip.shape[1:])


def sum_rows(values, axis):
    count = lax.axis_size(axis)
    chunks = values.reshape((count, values.shape[0] // count) + values.shape[1:])
    received = lax.all_to_all(chunks.astype(jnp.bfloat16), axis, 0, 0, tiled=True)
    return received.astype(jnp.float32).sum(axis=0)


def dft_tables(length):
    positions = jnp.arange(length, dtype=jnp.int32)
    angles = (positions[:, None] * positions[None, :] % length).astype(jnp.float32) * (
        2.0 * math.pi / length
    )
    norm_factor = 1.0 / math.sqrt(length)
    return (
        (jnp.cos(angles) * norm_factor).astype(jnp.bfloat16),
        (-jnp.sin(angles) * norm_factor).astype(jnp.bfloat16),
    )


def column_part(rounded, col_cat):
    row_count, source_count, col_count = rounded.shape
    product = jnp.dot(
        rounded.reshape(row_count * source_count, col_count),
        col_cat,
        preferred_element_type=jnp.float32,
    )
    return product.astype(jnp.bfloat16).reshape(row_count, source_count * 2 * col_count)


def combine_forward(real_prod, imag_prod, source_count, col_count):
    real_prod = real_prod.reshape(real_prod.shape[0], source_count, 2, col_count)
    imag_prod = imag_prod.reshape(imag_prod.shape[0], source_count, 2, col_count)
    real_out = real_prod[:, :, 0] - imag_prod[:, :, 1]
    imag_out = real_prod[:, :, 1] + imag_prod[:, :, 0]
    return jnp.stack([real_out, imag_out], axis=2)


def inverse_rows(row_real, row_imag, packed_grad, col_back, source_count, col_count):
    real_prod = jnp.dot(row_real, packed_grad, preferred_element_type=jnp.float32)
    imag_prod = jnp.dot(row_imag, packed_grad, preferred_element_type=jnp.float32)
    real_prod = real_prod.reshape(real_prod.shape[0], source_count, 2, col_count)
    imag_prod = imag_prod.reshape(imag_prod.shape[0], source_count, 2, col_count)
    real_out = real_prod[:, :, 0] + imag_prod[:, :, 1]
    imag_out = real_prod[:, :, 1] - imag_prod[:, :, 0]
    joined = jnp.concatenate([real_out, imag_out], axis=-1).astype(jnp.bfloat16)
    result = jnp.dot(
        joined.reshape(-1, 2 * col_count), col_back, preferred_element_type=jnp.float32
    )
    return result.reshape(real_prod.shape[0], source_count, col_count)


def block_gradient(fourier, data_block, beam_block, mix_block, level_block):
    predicted = jnp.einsum("ct,ktzl->kczl", mix_block, fourier)
    beam_gain = beam_block.astype(jnp.float32)[:, :, None, :]
    residual = data_block.astype(jnp.float32) - beam_gain * predicted
    weight = level_block.astype(jnp.float32) * 0.25
    weighted = weight[None, :, None, None] * beam_gain * residual
    summed = jnp.einsum("cs,kczl->kszl", mix_block, weighted)
    return summed.astype(jnp.bfloat16)


def smooth_rows(padded, spacing, row_count):
    return (
        padded[0:row_count]
        + 2.0 * padded[spacing : spacing + row_count]
        + padded[2 * spacing : 2 * spacing + row_count]
    ) * 0.25


def smooth_cols(values, spacing):
    padded = jnp.pad(values, ((0, 0), (0, 0), (spacing, spacing)))
    return (
        padded[..., : -2 * spacing]
        + 2.0 * padded[..., spacing:-spacing]
        + padded[..., 2 * spacing :]
    ) * 0.25


def shrink(values, bound_value):
    return values - jnp.clip(values, -bound_value, bound_value)


def combine_scales(updated, smooth_one, coarse, fine_bound, coarse_bound):
    return (
        coarse
        + shrink(smooth_one - coarse, coarse_bound)
        + shrink(updated - smooth_one, fine_bound)
    )


def body(sky_data, beam_gains, mixing, noise_levels, threshold_levels, start_sources):
    strip_rows, source_count, col_count = start_sources.shape
    full_rows = strip_rows * lax.axis_size("chan")
    row_real, row_imag = dft_tables(full_rows)
    col_real, col_imag = dft_tables(col_count)
    col_cat = jnp.concatenate([col_real, col_imag], axis=1)
    col_back = jnp.concatenate([col_real, col_imag], axis=0)
    bounds = threshold_levels.astype(jnp.float32) * 0.05
    fine_bound = bounds[:, 0][:, None]
    coarse_bound = bounds[:, 1][:, None]
    first_row = lax.axis_index("chan") * strip_rows
    sources = start_sources
    for iteration in range(ITERS):
        rounded = sources.astype(jnp.bfloat16)
        gather = gather_all if iteration == 0 else gather_rows
        gathered = gather(rounded, "chan")
        packed = column_part(gathered, col_cat)
        fourier = combine_forward(
            jnp.dot(row_real, packed, preferred_element_type=jnp.float32),
            jnp.dot(row_imag, packed, preferred_element_type=jnp.float32),
            source_count,
            col_count,
        )
        grad_local = block_gradient(fourier, sky_data, beam_gains, mixing, noise_levels)
        packed_grad = grad_local.reshape(full_rows, source_count * 2 * col_count)
        gradient = sum_rows(
            inverse_rows(row_real, row_imag, packed_grad, col_back, source_count, col_count),
            "chan",
        )
        updated = sources + gradient
        wide_pad = padded_2(updated, (("chan", 0),), 3)
        smooth_wide = smooth_cols(smooth_rows(wide_pad, 1, strip_rows + 4), 1)
        inside = (first_row - 2 + jnp.arange(strip_rows + 4) >= 0) & (
            first_row - 2 + jnp.arange(strip_rows + 4) < full_rows
        )
        smooth_wide = jnp.where(inside[:, None, None], smooth_wide, 0.0)
        smooth_one = smooth_wide[2 : 2 + strip_rows]
        coarse = smooth_cols(smooth_rows(smooth_wide, 2, strip_rows), 2)
        sources = combine_scales(updated, smooth_one, coarse, fine_bound, coarse_bound)
    return sources


def solution(mesh):
    return jax.shard_map(
        body,
        mesh=mesh,
        in_specs=(
            P("groups", "chan", None, None),
            P("groups", "chan", None),
            P(("groups", "chan"), None),
            P("chan"),
            P(),
            P(("groups", "chan"), None, None),
        ),
        out_specs=P(("groups", "chan"), None, None),
        check_vma=False,
    )
```

```python
import math

import jax
import jax.numpy as jnp
from jax import lax
from jax.sharding import PartitionSpec as P

ITERS = 2


def padded_2(cells, sides, width):
    for axis, dim in sides:
        count = lax.axis_size(axis)
        ends = count - 1
        head = lax.slice_in_dim(cells, 0, width, axis=dim)
        tail = lax.slice_in_dim(cells, cells.shape[dim] - width, cells.shape[dim], axis=dim)
        cells = jnp.concatenate(
            [
                lax.ppermute(tail, axis, [(i, (i + 1) % count) for i in range(ends)]),
                cells,
                lax.ppermute(head, axis, [((i + 1) % count, i) for i in range(ends)]),
            ],
            axis=dim,
        )
    return cells


def gather_all(strip, axis):
    count = lax.axis_size(axis)
    copies = jnp.broadcast_to(strip[None], (count,) + strip.shape)
    joined = lax.all_to_all(copies, axis, 0, 0, tiled=True)
    return joined.reshape((count * strip.shape[0],) + strip.shape[1:])


def gather_rows(strip, axis):
    count = lax.axis_size(axis)
    bits = count.bit_length() - 1
    assert 1 << bits == count
    own = lax.axis_index(axis)
    joined = strip
    for depth, bit in enumerate(reversed(range(bits))):
        partner = lax.ppermute(joined, axis, [(i, i ^ (1 << bit)) for i in range(count)])
        upper = ((own >> bit) & 1) == 1
        low = jnp.where(upper, partner, joined)
        high = jnp.where(upper, joined, partner)
        joined = jnp.stack([low, high], axis=depth)
    return joined.reshape((count * strip.shape[0],) + strip.shape[1:])


def sum_rows(values, axis):
    count = lax.axis_size(axis)
    bits = count.bit_length() - 1
    assert 1 << bits == count
    own = lax.axis_index(axis)
    split = values.reshape((2,) * bits + (values.shape[0] // count,) + values.shape[1:])
    for bit in range(bits):
        dim = bits - 1 - bit
        side = (own >> bit) & 1
        keep = lax.dynamic_index_in_dim(split, side, axis=dim, keepdims=False)
        send = lax.dynamic_index_in_dim(split, 1 - side, axis=dim, keepdims=False)
        moved = lax.ppermute(
            send.astype(jnp.bfloat16), axis, [(i, i ^ (1 << bit)) for i in range(count)]
        )
        split = keep + moved.astype(jnp.float32)
    return split


def dft_tables(length):
    positions = jnp.arange(length, dtype=jnp.int32)
    angles = (positions[:, None] * positions[None, :] % length).astype(jnp.float32) * (
        2.0 * math.pi / length
    )
    norm_factor = 1.0 / math.sqrt(length)
    return (
        (jnp.cos(angles) * norm_factor).astype(jnp.bfloat16),
        (-jnp.sin(angles) * norm_factor).astype(jnp.bfloat16),
    )


def column_part(rounded, col_cat):
    row_count, source_count, col_count = rounded.shape
    product = jnp.dot(
        rounded.reshape(row_count * source_count, col_count),
        col_cat,
        preferred_element_type=jnp.float32,
    )
    return product.astype(jnp.bfloat16).reshape(row_count, source_count * 2 * col_count)


def combine_forward(real_prod, imag_prod, source_count, col_count):
    real_prod = real_prod.reshape(real_prod.shape[0], source_count, 2, col_count)
    imag_prod = imag_prod.reshape(imag_prod.shape[0], source_count, 2, col_count)
    real_out = real_prod[:, :, 0] - imag_prod[:, :, 1]
    imag_out = real_prod[:, :, 1] + imag_prod[:, :, 0]
    return jnp.stack([real_out, imag_out], axis=2)


def inverse_rows(row_real, row_imag, packed_grad, col_back, source_count, col_count):
    real_prod = jnp.dot(row_real, packed_grad, preferred_element_type=jnp.float32)
    imag_prod = jnp.dot(row_imag, packed_grad, preferred_element_type=jnp.float32)
    real_prod = real_prod.reshape(real_prod.shape[0], source_count, 2, col_count)
    imag_prod = imag_prod.reshape(imag_prod.shape[0], source_count, 2, col_count)
    real_out = real_prod[:, :, 0] + imag_prod[:, :, 1]
    imag_out = real_prod[:, :, 1] - imag_prod[:, :, 0]
    joined = jnp.concatenate([real_out, imag_out], axis=-1).astype(jnp.bfloat16)
    result = jnp.dot(
        joined.reshape(-1, 2 * col_count), col_back, preferred_element_type=jnp.float32
    )
    return result.reshape(real_prod.shape[0], source_count, col_count)


def block_gradient(fourier, data_block, beam_block, mix_block, level_block):
    predicted = sum(
        mix_block[None, :, t, None, None] * fourier[:, t, None, :, :]
        for t in range(mix_block.shape[1])
    )
    beam_gain = beam_block.astype(jnp.float32)[:, :, None, :]
    residual = data_block.astype(jnp.float32) - beam_gain * predicted
    weight = level_block.astype(jnp.float32) * 0.25
    weighted = weight[None, :, None, None] * beam_gain * residual
    summed = jnp.einsum("cs,kczl->kszl", mix_block, weighted)
    return summed.astype(jnp.bfloat16)


def smooth_rows(padded, spacing, row_count):
    return (
        padded[0:row_count]
        + 2.0 * padded[spacing : spacing + row_count]
        + padded[2 * spacing : 2 * spacing + row_count]
    ) * 0.25


def smooth_cols(values, spacing):
    padded = jnp.pad(values, ((0, 0), (0, 0), (spacing, spacing)))
    return (
        padded[..., : -2 * spacing]
        + 2.0 * padded[..., spacing:-spacing]
        + padded[..., 2 * spacing :]
    ) * 0.25


def shrink(values, bound_value):
    return values - jnp.clip(values, -bound_value, bound_value)


def combine_scales(updated, smooth_one, coarse, fine_bound, coarse_bound):
    return (
        coarse
        + shrink(smooth_one - coarse, coarse_bound)
        + shrink(updated - smooth_one, fine_bound)
    )


def body(sky_data, beam_gains, mixing, noise_levels, threshold_levels, start_sources):
    strip_rows, source_count, col_count = start_sources.shape
    full_rows = strip_rows * lax.axis_size("chan")
    row_real, row_imag = dft_tables(full_rows)
    col_real, col_imag = dft_tables(col_count)
    col_cat = jnp.concatenate([col_real, col_imag], axis=1)
    col_back = jnp.concatenate([col_real, col_imag], axis=0)
    bounds = threshold_levels.astype(jnp.float32) * 0.05
    fine_bound = bounds[:, 0][:, None]
    coarse_bound = bounds[:, 1][:, None]
    first_row = lax.axis_index("chan") * strip_rows
    sources = start_sources
    for iteration in range(ITERS):
        rounded = sources.astype(jnp.bfloat16)
        gather = gather_all if iteration == 0 else gather_rows
        gathered = gather(rounded, "chan")
        packed = column_part(gathered, col_cat)
        fourier = combine_forward(
            jnp.dot(row_real, packed, preferred_element_type=jnp.float32),
            jnp.dot(row_imag, packed, preferred_element_type=jnp.float32),
            source_count,
            col_count,
        )
        grad_local = block_gradient(fourier, sky_data, beam_gains, mixing, noise_levels)
        packed_grad = grad_local.reshape(full_rows, source_count * 2 * col_count)
        gradient = sum_rows(
            inverse_rows(row_real, row_imag, packed_grad, col_back, source_count, col_count),
            "chan",
        )
        updated = sources + gradient
        wide_pad = padded_2(updated, (("chan", 0),), 3)
        smooth_wide = smooth_cols(smooth_rows(wide_pad, 1, strip_rows + 4), 1)
        inside = (first_row - 2 + jnp.arange(strip_rows + 4) >= 0) & (
            first_row - 2 + jnp.arange(strip_rows + 4) < full_rows
        )
        smooth_wide = jnp.where(inside[:, None, None], smooth_wide, 0.0)
        smooth_one = smooth_wide[2 : 2 + strip_rows]
        coarse = smooth_cols(smooth_rows(smooth_wide, 2, strip_rows), 2)
        sources = combine_scales(updated, smooth_one, coarse, fine_bound, coarse_bound)
    return sources


def solution(mesh):
    return jax.shard_map(
        body,
        mesh=mesh,
        in_specs=(
            P("groups", "chan", None, None),
            P("groups", "chan", None),
            P(("groups", "chan"), None),
            P("chan"),
            P(),
            P(("groups", "chan"), None, None),
        ),
        out_specs=P(("groups", "chan"), None, None),
        check_vma=False,
    )
```

```python
import math

import jax
import jax.numpy as jnp
from jax import lax
from jax.experimental import pallas as pl
from jax.sharding import PartitionSpec as P

ITERS = 2


def padded_2(cells, sides, width):
    for axis, dim in sides:
        count = lax.axis_size(axis)
        ends = count - 1
        head = lax.slice_in_dim(cells, 0, width, axis=dim)
        tail = lax.slice_in_dim(cells, cells.shape[dim] - width, cells.shape[dim], axis=dim)
        cells = jnp.concatenate(
            [
                lax.ppermute(tail, axis, [(i, (i + 1) % count) for i in range(ends)]),
                cells,
                lax.ppermute(head, axis, [((i + 1) % count, i) for i in range(ends)]),
            ],
            axis=dim,
        )
    return cells


def gather_all(strip, axis):
    count = lax.axis_size(axis)
    copies = jnp.broadcast_to(strip[None], (count,) + strip.shape)
    joined = lax.all_to_all(copies, axis, 0, 0, tiled=True)
    return joined.reshape((count * strip.shape[0],) + strip.shape[1:])


def gather_rows(strip, axis):
    count = lax.axis_size(axis)
    bits = count.bit_length() - 1
    assert 1 << bits == count
    own = lax.axis_index(axis)
    joined = strip
    for depth, bit in enumerate(reversed(range(bits))):
        partner = lax.ppermute(joined, axis, [(i, i ^ (1 << bit)) for i in range(count)])
        upper = ((own >> bit) & 1) == 1
        low = jnp.where(upper, partner, joined)
        high = jnp.where(upper, joined, partner)
        joined = jnp.stack([low, high], axis=depth)
    return joined.reshape((count * strip.shape[0],) + strip.shape[1:])


def sum_rows(values, axis):
    count = lax.axis_size(axis)
    bits = count.bit_length() - 1
    assert 1 << bits == count
    own = lax.axis_index(axis)
    split = values.reshape((2,) * bits + (values.shape[0] // count,) + values.shape[1:])
    for bit in range(bits):
        dim = bits - 1 - bit
        side = (own >> bit) & 1
        keep = lax.dynamic_index_in_dim(split, side, axis=dim, keepdims=False)
        send = lax.dynamic_index_in_dim(split, 1 - side, axis=dim, keepdims=False)
        moved = lax.ppermute(
            send.astype(jnp.bfloat16), axis, [(i, i ^ (1 << bit)) for i in range(count)]
        )
        split = keep + moved.astype(jnp.float32)
    return split


def dft_tables(length):
    positions = jnp.arange(length, dtype=jnp.int32)
    angles = (positions[:, None] * positions[None, :] % length).astype(jnp.float32) * (
        2.0 * math.pi / length
    )
    norm_factor = 1.0 / math.sqrt(length)
    return (
        (jnp.cos(angles) * norm_factor).astype(jnp.bfloat16),
        (-jnp.sin(angles) * norm_factor).astype(jnp.bfloat16),
    )


def column_part(rounded, col_cat):
    row_count, source_count, col_count = rounded.shape
    product = jnp.dot(
        rounded.reshape(row_count * source_count, col_count),
        col_cat,
        preferred_element_type=jnp.float32,
    )
    return product.astype(jnp.bfloat16).reshape(row_count, source_count * 2 * col_count)


def combine_forward(real_prod, imag_prod, source_count, col_count):
    real_prod = real_prod.reshape(real_prod.shape[0], source_count, 2, col_count)
    imag_prod = imag_prod.reshape(imag_prod.shape[0], source_count, 2, col_count)
    real_out = real_prod[:, :, 0] - imag_prod[:, :, 1]
    imag_out = real_prod[:, :, 1] + imag_prod[:, :, 0]
    return jnp.stack([real_out, imag_out], axis=2)


def inverse_rows(row_real, row_imag, packed_grad, col_back, source_count, col_count):
    real_prod = jnp.dot(row_real, packed_grad, preferred_element_type=jnp.float32)
    imag_prod = jnp.dot(row_imag, packed_grad, preferred_element_type=jnp.float32)
    real_prod = real_prod.reshape(real_prod.shape[0], source_count, 2, col_count)
    imag_prod = imag_prod.reshape(imag_prod.shape[0], source_count, 2, col_count)
    real_out = real_prod[:, :, 0] + imag_prod[:, :, 1]
    imag_out = real_prod[:, :, 1] - imag_prod[:, :, 0]
    joined = jnp.concatenate([real_out, imag_out], axis=-1).astype(jnp.bfloat16)
    result = jnp.dot(
        joined.reshape(-1, 2 * col_count), col_back, preferred_element_type=jnp.float32
    )
    return result.reshape(real_prod.shape[0], source_count, col_count)


def gradient_kernel(mix_ref, wm_ref, q_ref, sky_ref, beam_ref, out_ref):
    mix = mix_ref[...]
    wm = wm_ref[...]
    fourier = q_ref[...]
    data = sky_ref[...].astype(jnp.float32)
    beam = beam_ref[...].astype(jnp.float32)
    beam = jnp.concatenate([beam, beam], axis=-1)
    predicted = mix[None, :, 0:1] * fourier[:, 0:1, :]
    for t in range(1, mix.shape[1]):
        predicted = predicted + mix[None, :, t : t + 1] * fourier[:, t : t + 1, :]
    beamed = beam * (data - beam * predicted)
    rows = [
        jnp.sum(wm[None, :, s : s + 1] * beamed, axis=1, keepdims=True) for s in range(wm.shape[1])
    ]
    out_ref[...] = jnp.concatenate(rows, axis=1).astype(out_ref.dtype)

def block_gradient(fourier, data_block, beam_block, mix_block, level_block, rows_per_step=8):
    row_count, chan_count, _, col_count = data_block.shape
    source_count = mix_block.shape[1]
    width = 2 * col_count
    weighted_mix = mix_block * (level_block.astype(jnp.float32) * 0.25)[:, None]
    out = pl.pallas_call(
        gradient_kernel,
        grid=(row_count // rows_per_step,),
        in_specs=[
            pl.BlockSpec((chan_count, source_count), lambda i: (0, 0)),
            pl.BlockSpec((chan_count, source_count), lambda i: (0, 0)),
            pl.BlockSpec((rows_per_step, source_count, width), lambda i: (i, 0, 0)),
            pl.BlockSpec((rows_per_step, chan_count, width), lambda i: (i, 0, 0)),
            pl.BlockSpec((rows_per_step, chan_count, col_count), lambda i: (i, 0, 0)),
        ],
        out_specs=pl.BlockSpec((rows_per_step, source_count, width), lambda i: (i, 0, 0)),
        out_shape=jax.ShapeDtypeStruct((row_count, source_count, width), jnp.bfloat16),
    )(
        mix_block,
        weighted_mix,
        fourier.reshape(row_count, source_count, width),
        data_block.reshape(row_count, chan_count, width),
        beam_block,
    )
    return out

def smooth_rows(padded, spacing, row_count):
    return (
        padded[0:row_count]
        + 2.0 * padded[spacing : spacing + row_count]
        + padded[2 * spacing : 2 * spacing + row_count]
    ) * 0.25


def smooth_cols(values, spacing):
    padded = jnp.pad(values, ((0, 0), (0, 0), (spacing, spacing)))
    return (
        padded[..., : -2 * spacing]
        + 2.0 * padded[..., spacing:-spacing]
        + padded[..., 2 * spacing :]
    ) * 0.25


def shrink(values, bound_value):
    return values - jnp.clip(values, -bound_value, bound_value)


def combine_scales(updated, smooth_one, coarse, fine_bound, coarse_bound):
    return (
        coarse
        + shrink(smooth_one - coarse, coarse_bound)
        + shrink(updated - smooth_one, fine_bound)
    )


def body(sky_data, beam_gains, mixing, noise_levels, threshold_levels, start_sources):
    strip_rows, source_count, col_count = start_sources.shape
    full_rows = strip_rows * lax.axis_size("chan")
    row_real, row_imag = dft_tables(full_rows)
    col_real, col_imag = dft_tables(col_count)
    col_cat = jnp.concatenate([col_real, col_imag], axis=1)
    col_back = jnp.concatenate([col_real, col_imag], axis=0)
    bounds = threshold_levels.astype(jnp.float32) * 0.05
    fine_bound = bounds[:, 0][:, None]
    coarse_bound = bounds[:, 1][:, None]
    first_row = lax.axis_index("chan") * strip_rows
    sources = start_sources
    for iteration in range(ITERS):
        rounded = sources.astype(jnp.bfloat16)
        gather = gather_all if iteration == 0 else gather_rows
        gathered = gather(rounded, "chan")
        packed = column_part(gathered, col_cat)
        fourier = combine_forward(
            jnp.dot(row_real, packed, preferred_element_type=jnp.float32),
            jnp.dot(row_imag, packed, preferred_element_type=jnp.float32),
            source_count,
            col_count,
        )
        grad_local = block_gradient(fourier, sky_data, beam_gains, mixing, noise_levels)
        packed_grad = grad_local.reshape(full_rows, source_count * 2 * col_count)
        gradient = sum_rows(
            inverse_rows(row_real, row_imag, packed_grad, col_back, source_count, col_count),
            "chan",
        )
        updated = sources + gradient
        wide_pad = padded_2(updated, (("chan", 0),), 3)
        smooth_wide = smooth_cols(smooth_rows(wide_pad, 1, strip_rows + 4), 1)
        inside = (first_row - 2 + jnp.arange(strip_rows + 4) >= 0) & (
            first_row - 2 + jnp.arange(strip_rows + 4) < full_rows
        )
        smooth_wide = jnp.where(inside[:, None, None], smooth_wide, 0.0)
        smooth_one = smooth_wide[2 : 2 + strip_rows]
        coarse = smooth_cols(smooth_rows(smooth_wide, 2, strip_rows), 2)
        sources = combine_scales(updated, smooth_one, coarse, fine_bound, coarse_bound)
    return sources


def solution(mesh):
    return jax.shard_map(
        body,
        mesh=mesh,
        in_specs=(
            P("groups", "chan", None, None),
            P("groups", "chan", None),
            P(("groups", "chan"), None),
            P("chan"),
            P(),
            P(("groups", "chan"), None, None),
        ),
        out_specs=P(("groups", "chan"), None, None),
        check_vma=False,
    )
```

```python
import math

import jax
import jax.numpy as jnp
from jax import lax
from jax.experimental import pallas as pl
from jax.sharding import PartitionSpec as P

ITERS = 2


def padded_2(cells, sides, width):
    for axis, dim in sides:
        count = lax.axis_size(axis)
        ends = count - 1
        head = lax.slice_in_dim(cells, 0, width, axis=dim)
        tail = lax.slice_in_dim(cells, cells.shape[dim] - width, cells.shape[dim], axis=dim)
        cells = jnp.concatenate(
            [
                lax.ppermute(tail, axis, [(i, (i + 1) % count) for i in range(ends)]),
                cells,
                lax.ppermute(head, axis, [((i + 1) % count, i) for i in range(ends)]),
            ],
            axis=dim,
        )
    return cells


def gather_all(strip, axis):
    count = lax.axis_size(axis)
    copies = jnp.broadcast_to(strip[None], (count,) + strip.shape)
    joined = lax.all_to_all(copies, axis, 0, 0, tiled=True)
    return joined.reshape((count * strip.shape[0],) + strip.shape[1:])


def gather_rows(strip, axis):
    count = lax.axis_size(axis)
    bits = count.bit_length() - 1
    assert 1 << bits == count
    own = lax.axis_index(axis)
    joined = strip
    for depth, bit in enumerate(reversed(range(bits))):
        partner = lax.ppermute(joined, axis, [(i, i ^ (1 << bit)) for i in range(count)])
        upper = ((own >> bit) & 1) == 1
        low = jnp.where(upper, partner, joined)
        high = jnp.where(upper, joined, partner)
        joined = jnp.stack([low, high], axis=depth)
    return joined.reshape((count * strip.shape[0],) + strip.shape[1:])


def sum_rows(values, axis):
    count = lax.axis_size(axis)
    bits = count.bit_length() - 1
    assert 1 << bits == count
    own = lax.axis_index(axis)
    split = values.reshape((2,) * bits + (values.shape[0] // count,) + values.shape[1:])
    for bit in range(bits):
        dim = bits - 1 - bit
        side = (own >> bit) & 1
        keep = lax.dynamic_index_in_dim(split, side, axis=dim, keepdims=False)
        send = lax.dynamic_index_in_dim(split, 1 - side, axis=dim, keepdims=False)
        moved = lax.ppermute(
            send.astype(jnp.bfloat16), axis, [(i, i ^ (1 << bit)) for i in range(count)]
        )
        split = keep + moved.astype(jnp.float32)
    return split


def dft_tables(length):
    positions = jnp.arange(length, dtype=jnp.int32)
    angles = (positions[:, None] * positions[None, :] % length).astype(jnp.float32) * (
        2.0 * math.pi / length
    )
    norm_factor = 1.0 / math.sqrt(length)
    return (
        (jnp.cos(angles) * norm_factor).astype(jnp.bfloat16),
        (-jnp.sin(angles) * norm_factor).astype(jnp.bfloat16),
    )


def column_part(rounded, col_cat):
    row_count, source_count, col_count = rounded.shape
    product = jnp.dot(
        rounded.reshape(row_count * source_count, col_count),
        col_cat,
        preferred_element_type=jnp.float32,
    )
    return product.astype(jnp.bfloat16).reshape(row_count, source_count * 2 * col_count)


def combine_forward(real_prod, imag_prod, source_count, col_count):
    real_prod = real_prod.reshape(real_prod.shape[0], source_count, 2, col_count)
    imag_prod = imag_prod.reshape(imag_prod.shape[0], source_count, 2, col_count)
    real_out = real_prod[:, :, 0] - imag_prod[:, :, 1]
    imag_out = real_prod[:, :, 1] + imag_prod[:, :, 0]
    return jnp.stack([real_out, imag_out], axis=2)


def inverse_rows(row_real, row_imag, packed_grad, col_back, source_count, col_count):
    real_prod = jnp.dot(row_real, packed_grad, preferred_element_type=jnp.float32)
    imag_prod = jnp.dot(row_imag, packed_grad, preferred_element_type=jnp.float32)
    real_prod = real_prod.reshape(real_prod.shape[0], source_count, 2, col_count)
    imag_prod = imag_prod.reshape(imag_prod.shape[0], source_count, 2, col_count)
    real_out = real_prod[:, :, 0] + imag_prod[:, :, 1]
    imag_out = real_prod[:, :, 1] - imag_prod[:, :, 0]
    joined = jnp.concatenate([real_out, imag_out], axis=-1).astype(jnp.bfloat16)
    result = jnp.dot(
        joined.reshape(-1, 2 * col_count), col_back, preferred_element_type=jnp.float32
    )
    return result.reshape(real_prod.shape[0], source_count, col_count)


def gradient_kernel(spread_ref, gather_ref, q_ref, sky_ref, beam_ref, out_ref):
    source_count, rows, width = q_ref.shape
    chan_count = sky_ref.shape[1]
    fourier = q_ref[...].reshape(source_count * rows, width)
    predicted = lax.dot(
        spread_ref[...], fourier, precision=lax.Precision.HIGHEST,
        preferred_element_type=jnp.float32,
    ).reshape(rows, chan_count, width)
    beam = beam_ref[...].astype(jnp.float32)
    beam = jnp.concatenate([beam, beam], axis=-1)
    beamed = beam * (sky_ref[...].astype(jnp.float32) - beam * predicted)
    summed = lax.dot(
        gather_ref[...], beamed.reshape(rows * chan_count, width),
        precision=lax.Precision.HIGHEST, preferred_element_type=jnp.float32,
    )
    out_ref[...] = summed.reshape(source_count, rows, width).astype(out_ref.dtype)

def block_gradient(fourier, data_block, beam_block, mix_block, level_block, rows_per_step=8):
    row_count, chan_count, _, col_count = data_block.shape
    source_count = mix_block.shape[1]
    width = 2 * col_count
    weighted_mix = mix_block * (level_block.astype(jnp.float32) * 0.25)[:, None]
    eye = jnp.eye(rows_per_step, dtype=jnp.float32)
    spread = (eye[:, None, None, :] * mix_block[None, :, :, None]).reshape(
        rows_per_step * chan_count, source_count * rows_per_step)
    gather = (eye[None, :, :, None] * weighted_mix.T[:, None, None, :]).reshape(
        source_count * rows_per_step, rows_per_step * chan_count)
    by_source = jnp.transpose(fourier.reshape(row_count, source_count, width), (1, 0, 2))
    out = pl.pallas_call(
        gradient_kernel,
        grid=(row_count // rows_per_step,),
        in_specs=[
            pl.BlockSpec(spread.shape, lambda i: (0, 0)),
            pl.BlockSpec(gather.shape, lambda i: (0, 0)),
            pl.BlockSpec((source_count, rows_per_step, width), lambda i: (0, i, 0)),
            pl.BlockSpec((rows_per_step, chan_count, width), lambda i: (i, 0, 0)),
            pl.BlockSpec((rows_per_step, chan_count, col_count), lambda i: (i, 0, 0)),
        ],
        out_specs=pl.BlockSpec((source_count, rows_per_step, width), lambda i: (0, i, 0)),
        out_shape=jax.ShapeDtypeStruct((source_count, row_count, width), jnp.bfloat16),
    )(spread, gather, by_source, data_block.reshape(row_count, chan_count, width), beam_block)
    return jnp.transpose(out, (1, 0, 2))

def smooth_rows(padded, spacing, row_count):
    return (
        padded[0:row_count]
        + 2.0 * padded[spacing : spacing + row_count]
        + padded[2 * spacing : 2 * spacing + row_count]
    ) * 0.25


def smooth_cols(values, spacing):
    padded = jnp.pad(values, ((0, 0), (0, 0), (spacing, spacing)))
    return (
        padded[..., : -2 * spacing]
        + 2.0 * padded[..., spacing:-spacing]
        + padded[..., 2 * spacing :]
    ) * 0.25


def shrink(values, bound_value):
    return values - jnp.clip(values, -bound_value, bound_value)


def combine_scales(updated, smooth_one, coarse, fine_bound, coarse_bound):
    return (
        coarse
        + shrink(smooth_one - coarse, coarse_bound)
        + shrink(updated - smooth_one, fine_bound)
    )


def body(sky_data, beam_gains, mixing, noise_levels, threshold_levels, start_sources):
    strip_rows, source_count, col_count = start_sources.shape
    full_rows = strip_rows * lax.axis_size("chan")
    row_real, row_imag = dft_tables(full_rows)
    col_real, col_imag = dft_tables(col_count)
    col_cat = jnp.concatenate([col_real, col_imag], axis=1)
    col_back = jnp.concatenate([col_real, col_imag], axis=0)
    bounds = threshold_levels.astype(jnp.float32) * 0.05
    fine_bound = bounds[:, 0][:, None]
    coarse_bound = bounds[:, 1][:, None]
    first_row = lax.axis_index("chan") * strip_rows
    sources = start_sources
    for iteration in range(ITERS):
        rounded = sources.astype(jnp.bfloat16)
        gather = gather_all if iteration == 0 else gather_rows
        gathered = gather(rounded, "chan")
        packed = column_part(gathered, col_cat)
        fourier = combine_forward(
            jnp.dot(row_real, packed, preferred_element_type=jnp.float32),
            jnp.dot(row_imag, packed, preferred_element_type=jnp.float32),
            source_count,
            col_count,
        )
        grad_local = block_gradient(fourier, sky_data, beam_gains, mixing, noise_levels)
        packed_grad = grad_local.reshape(full_rows, source_count * 2 * col_count)
        gradient = sum_rows(
            inverse_rows(row_real, row_imag, packed_grad, col_back, source_count, col_count),
            "chan",
        )
        updated = sources + gradient
        wide_pad = padded_2(updated, (("chan", 0),), 3)
        smooth_wide = smooth_cols(smooth_rows(wide_pad, 1, strip_rows + 4), 1)
        inside = (first_row - 2 + jnp.arange(strip_rows + 4) >= 0) & (
            first_row - 2 + jnp.arange(strip_rows + 4) < full_rows
        )
        smooth_wide = jnp.where(inside[:, None, None], smooth_wide, 0.0)
        smooth_one = smooth_wide[2 : 2 + strip_rows]
        coarse = smooth_cols(smooth_rows(smooth_wide, 2, strip_rows), 2)
        sources = combine_scales(updated, smooth_one, coarse, fine_bound, coarse_bound)
    return sources


def solution(mesh):
    return jax.shard_map(
        body,
        mesh=mesh,
        in_specs=(
            P("groups", "chan", None, None),
            P("groups", "chan", None),
            P(("groups", "chan"), None),
            P("chan"),
            P(),
            P(("groups", "chan"), None, None),
        ),
        out_specs=P(("groups", "chan"), None, None),
        check_vma=False,
    )
```

```python
import math

import jax
import jax.numpy as jnp
from jax import lax
from jax.sharding import PartitionSpec as P

ITERS = 2


def padded_2(cells, sides, width):
    for axis, dim in sides:
        count = lax.axis_size(axis)
        ends = count - 1
        head = lax.slice_in_dim(cells, 0, width, axis=dim)
        tail = lax.slice_in_dim(cells, cells.shape[dim] - width, cells.shape[dim], axis=dim)
        cells = jnp.concatenate(
            [
                lax.ppermute(tail, axis, [(i, (i + 1) % count) for i in range(ends)]),
                cells,
                lax.ppermute(head, axis, [((i + 1) % count, i) for i in range(ends)]),
            ],
            axis=dim,
        )
    return cells


def gather_all(strip, axis):
    count = lax.axis_size(axis)
    copies = jnp.broadcast_to(strip[None], (count,) + strip.shape)
    joined = lax.all_to_all(copies, axis, 0, 0, tiled=True)
    return joined.reshape((count * strip.shape[0],) + strip.shape[1:])


def gather_rows(strip, axis):
    count = lax.axis_size(axis)
    bits = count.bit_length() - 1
    assert 1 << bits == count
    own = lax.axis_index(axis)
    joined = strip
    for depth, bit in enumerate(reversed(range(bits))):
        partner = lax.ppermute(joined, axis, [(i, i ^ (1 << bit)) for i in range(count)])
        upper = ((own >> bit) & 1) == 1
        low = jnp.where(upper, partner, joined)
        high = jnp.where(upper, joined, partner)
        joined = jnp.stack([low, high], axis=depth)
    return joined.reshape((count * strip.shape[0],) + strip.shape[1:])


def sum_rows(values, axis):
    count = lax.axis_size(axis)
    half = count // 2
    parity = lax.axis_index(axis) % 2
    strip = values.shape[0] // count
    pairs = values.reshape((half, 2, strip) + values.shape[1:])
    even = pairs[:, 0]
    odd = pairs[:, 1]
    keep = jnp.where(parity == 1, odd, even)
    send = jnp.where(parity == 1, even, odd)
    moved = lax.ppermute(
        send.astype(jnp.bfloat16), axis, [(i, i ^ 1) for i in range(count)]
    )
    chip_sum = (keep + moved.astype(jnp.float32)).astype(jnp.bfloat16)
    groups = [list(range(p, count, 2)) for p in range(2)]
    received = lax.all_to_all(chip_sum, axis, 0, 0, tiled=True, axis_index_groups=groups)
    return received.astype(jnp.float32).sum(axis=0)


def dft_tables(length):
    positions = jnp.arange(length, dtype=jnp.int32)
    angles = (positions[:, None] * positions[None, :] % length).astype(jnp.float32) * (
        2.0 * math.pi / length
    )
    norm_factor = 1.0 / math.sqrt(length)
    return (
        (jnp.cos(angles) * norm_factor).astype(jnp.bfloat16),
        (-jnp.sin(angles) * norm_factor).astype(jnp.bfloat16),
    )


def column_part(rounded, col_cat):
    row_count, source_count, col_count = rounded.shape
    product = jnp.dot(
        rounded.reshape(row_count * source_count, col_count),
        col_cat,
        preferred_element_type=jnp.float32,
    )
    return product.astype(jnp.bfloat16).reshape(row_count, source_count * 2 * col_count)


def combine_forward(real_prod, imag_prod, source_count, col_count):
    real_prod = real_prod.reshape(real_prod.shape[0], source_count, 2, col_count)
    imag_prod = imag_prod.reshape(imag_prod.shape[0], source_count, 2, col_count)
    real_out = real_prod[:, :, 0] - imag_prod[:, :, 1]
    imag_out = real_prod[:, :, 1] + imag_prod[:, :, 0]
    return jnp.stack([real_out, imag_out], axis=2)


def inverse_rows(row_real, row_imag, packed_grad, col_back, source_count, col_count):
    real_prod = jnp.dot(row_real, packed_grad, preferred_element_type=jnp.float32)
    imag_prod = jnp.dot(row_imag, packed_grad, preferred_element_type=jnp.float32)
    real_prod = real_prod.reshape(real_prod.shape[0], source_count, 2, col_count)
    imag_prod = imag_prod.reshape(imag_prod.shape[0], source_count, 2, col_count)
    real_out = real_prod[:, :, 0] + imag_prod[:, :, 1]
    imag_out = real_prod[:, :, 1] - imag_prod[:, :, 0]
    joined = jnp.concatenate([real_out, imag_out], axis=-1).astype(jnp.bfloat16)
    result = jnp.dot(
        joined.reshape(-1, 2 * col_count), col_back, preferred_element_type=jnp.float32
    )
    return result.reshape(real_prod.shape[0], source_count, col_count)


def block_gradient(fourier, data_block, beam_block, mix_block, level_block):
    predicted = jnp.einsum("ct,ktzl->kczl", mix_block, fourier)
    beam_gain = beam_block.astype(jnp.float32)[:, :, None, :]
    residual = data_block.astype(jnp.float32) - beam_gain * predicted
    weight = level_block.astype(jnp.float32) * 0.25
    weighted = weight[None, :, None, None] * beam_gain * residual
    summed = jnp.einsum("cs,kczl->kszl", mix_block, weighted)
    return summed.astype(jnp.bfloat16)


def smooth_rows(padded, spacing, row_count):
    return (
        padded[0:row_count]
        + 2.0 * padded[spacing : spacing + row_count]
        + padded[2 * spacing : 2 * spacing + row_count]
    ) * 0.25


def smooth_cols(values, spacing):
    padded = jnp.pad(values, ((0, 0), (0, 0), (spacing, spacing)))
    return (
        padded[..., : -2 * spacing]
        + 2.0 * padded[..., spacing:-spacing]
        + padded[..., 2 * spacing :]
    ) * 0.25


def shrink(values, bound_value):
    return values - jnp.clip(values, -bound_value, bound_value)


def combine_scales(updated, smooth_one, coarse, fine_bound, coarse_bound):
    return (
        coarse
        + shrink(smooth_one - coarse, coarse_bound)
        + shrink(updated - smooth_one, fine_bound)
    )


def body(sky_data, beam_gains, mixing, noise_levels, threshold_levels, start_sources):
    strip_rows, source_count, col_count = start_sources.shape
    full_rows = strip_rows * lax.axis_size("chan")
    row_real, row_imag = dft_tables(full_rows)
    col_real, col_imag = dft_tables(col_count)
    col_cat = jnp.concatenate([col_real, col_imag], axis=1)
    col_back = jnp.concatenate([col_real, col_imag], axis=0)
    bounds = threshold_levels.astype(jnp.float32) * 0.05
    fine_bound = bounds[:, 0][:, None]
    coarse_bound = bounds[:, 1][:, None]
    first_row = lax.axis_index("chan") * strip_rows
    sources = start_sources
    for iteration in range(ITERS):
        rounded = sources.astype(jnp.bfloat16)
        gather = gather_all if iteration == 0 else gather_rows
        gathered = gather(rounded, "chan")
        packed = column_part(gathered, col_cat)
        fourier = combine_forward(
            jnp.dot(row_real, packed, preferred_element_type=jnp.float32),
            jnp.dot(row_imag, packed, preferred_element_type=jnp.float32),
            source_count,
            col_count,
        )
        grad_local = block_gradient(fourier, sky_data, beam_gains, mixing, noise_levels)
        packed_grad = grad_local.reshape(full_rows, source_count * 2 * col_count)
        gradient = sum_rows(
            inverse_rows(row_real, row_imag, packed_grad, col_back, source_count, col_count),
            "chan",
        )
        updated = sources + gradient
        wide_pad = padded_2(updated, (("chan", 0),), 3)
        smooth_wide = smooth_cols(smooth_rows(wide_pad, 1, strip_rows + 4), 1)
        inside = (first_row - 2 + jnp.arange(strip_rows + 4) >= 0) & (
            first_row - 2 + jnp.arange(strip_rows + 4) < full_rows
        )
        smooth_wide = jnp.where(inside[:, None, None], smooth_wide, 0.0)
        smooth_one = smooth_wide[2 : 2 + strip_rows]
        coarse = smooth_cols(smooth_rows(smooth_wide, 2, strip_rows), 2)
        sources = combine_scales(updated, smooth_one, coarse, fine_bound, coarse_bound)
    return sources


def solution(mesh):
    return jax.shard_map(
        body,
        mesh=mesh,
        in_specs=(
            P("groups", "chan", None, None),
            P("groups", "chan", None),
            P(("groups", "chan"), None),
            P("chan"),
            P(),
            P(("groups", "chan"), None, None),
        ),
        out_specs=P(("groups", "chan"), None, None),
        check_vma=False,
    )
```

```python
import math

import jax
import jax.numpy as jnp
from jax import lax
from jax.sharding import PartitionSpec as P

ITERS = 2


def padded_2(cells, sides, width):
    for axis, dim in sides:
        count = lax.axis_size(axis)
        ends = count - 1
        head = lax.slice_in_dim(cells, 0, width, axis=dim)
        tail = lax.slice_in_dim(cells, cells.shape[dim] - width, cells.shape[dim], axis=dim)
        cells = jnp.concatenate(
            [
                lax.ppermute(tail, axis, [(i, (i + 1) % count) for i in range(ends)]),
                cells,
                lax.ppermute(head, axis, [((i + 1) % count, i) for i in range(ends)]),
            ],
            axis=dim,
        )
    return cells


def gather_rows(strip, axis):
    count = lax.axis_size(axis)
    half = count // 2
    parity = lax.axis_index(axis) % 2
    groups = [list(range(p, count, 2)) for p in range(2)]
    copies = jnp.broadcast_to(strip[None], (half,) + strip.shape)
    own_side = lax.all_to_all(copies, axis, 0, 0, tiled=True, axis_index_groups=groups)
    other_side = lax.ppermute(own_side, axis, [(i, i ^ 1) for i in range(count)])
    even = jnp.where(parity == 1, other_side, own_side)
    odd = jnp.where(parity == 1, own_side, other_side)
    joined = jnp.stack([even, odd], axis=1)
    return joined.reshape((count * strip.shape[0],) + strip.shape[1:])


def sum_rows(values, axis):
    count = lax.axis_size(axis)
    half = count // 2
    parity = lax.axis_index(axis) % 2
    strip = values.shape[0] // count
    pairs = values.reshape((half, 2, strip) + values.shape[1:])
    even = pairs[:, 0]
    odd = pairs[:, 1]
    keep = jnp.where(parity == 1, odd, even)
    send = jnp.where(parity == 1, even, odd)
    moved = lax.ppermute(
        send.astype(jnp.bfloat16), axis, [(i, i ^ 1) for i in range(count)]
    )
    chip_sum = (keep + moved.astype(jnp.float32)).astype(jnp.bfloat16)
    groups = [list(range(p, count, 2)) for p in range(2)]
    received = lax.all_to_all(chip_sum, axis, 0, 0, tiled=True, axis_index_groups=groups)
    return received.astype(jnp.float32).sum(axis=0)


def dft_tables(length):
    positions = jnp.arange(length, dtype=jnp.int32)
    angles = (positions[:, None] * positions[None, :] % length).astype(jnp.float32) * (
        2.0 * math.pi / length
    )
    norm_factor = 1.0 / math.sqrt(length)
    return (
        (jnp.cos(angles) * norm_factor).astype(jnp.bfloat16),
        (-jnp.sin(angles) * norm_factor).astype(jnp.bfloat16),
    )


def column_part(rounded, col_cat):
    row_count, source_count, col_count = rounded.shape
    product = jnp.dot(
        rounded.reshape(row_count * source_count, col_count),
        col_cat,
        preferred_element_type=jnp.float32,
    )
    return product.astype(jnp.bfloat16).reshape(row_count, source_count * 2 * col_count)


def combine_forward(real_prod, imag_prod, source_count, col_count):
    real_prod = real_prod.reshape(real_prod.shape[0], source_count, 2, col_count)
    imag_prod = imag_prod.reshape(imag_prod.shape[0], source_count, 2, col_count)
    real_out = real_prod[:, :, 0] - imag_prod[:, :, 1]
    imag_out = real_prod[:, :, 1] + imag_prod[:, :, 0]
    return jnp.stack([real_out, imag_out], axis=2)


def inverse_rows(row_real, row_imag, packed_grad, col_back, source_count, col_count):
    real_prod = jnp.dot(row_real, packed_grad, preferred_element_type=jnp.float32)
    imag_prod = jnp.dot(row_imag, packed_grad, preferred_element_type=jnp.float32)
    real_prod = real_prod.reshape(real_prod.shape[0], source_count, 2, col_count)
    imag_prod = imag_prod.reshape(imag_prod.shape[0], source_count, 2, col_count)
    real_out = real_prod[:, :, 0] + imag_prod[:, :, 1]
    imag_out = real_prod[:, :, 1] - imag_prod[:, :, 0]
    joined = jnp.concatenate([real_out, imag_out], axis=-1).astype(jnp.bfloat16)
    result = jnp.dot(
        joined.reshape(-1, 2 * col_count), col_back, preferred_element_type=jnp.float32
    )
    return result.reshape(real_prod.shape[0], source_count, col_count)


def block_gradient(fourier, data_block, beam_block, mix_block, level_block):
    predicted = jnp.einsum("ct,ktzl->kczl", mix_block, fourier)
    beam_gain = beam_block.astype(jnp.float32)[:, :, None, :]
    residual = data_block.astype(jnp.float32) - beam_gain * predicted
    weight = level_block.astype(jnp.float32) * 0.25
    weighted = weight[None, :, None, None] * beam_gain * residual
    summed = jnp.einsum("cs,kczl->kszl", mix_block, weighted)
    return summed.astype(jnp.bfloat16)


def smooth_rows(padded, spacing, row_count):
    return (
        padded[0:row_count]
        + 2.0 * padded[spacing : spacing + row_count]
        + padded[2 * spacing : 2 * spacing + row_count]
    ) * 0.25


def smooth_cols(values, spacing):
    padded = jnp.pad(values, ((0, 0), (0, 0), (spacing, spacing)))
    return (
        padded[..., : -2 * spacing]
        + 2.0 * padded[..., spacing:-spacing]
        + padded[..., 2 * spacing :]
    ) * 0.25


def shrink(values, bound_value):
    return values - jnp.clip(values, -bound_value, bound_value)


def combine_scales(updated, smooth_one, coarse, fine_bound, coarse_bound):
    return (
        coarse
        + shrink(smooth_one - coarse, coarse_bound)
        + shrink(updated - smooth_one, fine_bound)
    )


def body(sky_data, beam_gains, mixing, noise_levels, threshold_levels, start_sources):
    strip_rows, source_count, col_count = start_sources.shape
    full_rows = strip_rows * lax.axis_size("chan")
    row_real, row_imag = dft_tables(full_rows)
    col_real, col_imag = dft_tables(col_count)
    col_cat = jnp.concatenate([col_real, col_imag], axis=1)
    col_back = jnp.concatenate([col_real, col_imag], axis=0)
    bounds = threshold_levels.astype(jnp.float32) * 0.05
    fine_bound = bounds[:, 0][:, None]
    coarse_bound = bounds[:, 1][:, None]
    first_row = lax.axis_index("chan") * strip_rows
    sources = start_sources
    for iteration in range(ITERS):
        rounded = sources.astype(jnp.bfloat16)
        gathered = gather_rows(rounded, "chan")
        packed = column_part(gathered, col_cat)
        fourier = combine_forward(
            jnp.dot(row_real, packed, preferred_element_type=jnp.float32),
            jnp.dot(row_imag, packed, preferred_element_type=jnp.float32),
            source_count,
            col_count,
        )
        grad_local = block_gradient(fourier, sky_data, beam_gains, mixing, noise_levels)
        packed_grad = grad_local.reshape(full_rows, source_count * 2 * col_count)
        gradient = sum_rows(
            inverse_rows(row_real, row_imag, packed_grad, col_back, source_count, col_count),
            "chan",
        )
        updated = sources + gradient
        wide_pad = padded_2(updated, (("chan", 0),), 3)
        smooth_wide = smooth_cols(smooth_rows(wide_pad, 1, strip_rows + 4), 1)
        inside = (first_row - 2 + jnp.arange(strip_rows + 4) >= 0) & (
            first_row - 2 + jnp.arange(strip_rows + 4) < full_rows
        )
        smooth_wide = jnp.where(inside[:, None, None], smooth_wide, 0.0)
        smooth_one = smooth_wide[2 : 2 + strip_rows]
        coarse = smooth_cols(smooth_rows(smooth_wide, 2, strip_rows), 2)
        sources = combine_scales(updated, smooth_one, coarse, fine_bound, coarse_bound)
    return sources


def solution(mesh):
    return jax.shard_map(
        body,
        mesh=mesh,
        in_specs=(
            P("groups", "chan", None, None),
            P("groups", "chan", None),
            P(("groups", "chan"), None),
            P("chan"),
            P(),
            P(("groups", "chan"), None, None),
        ),
        out_specs=P(("groups", "chan"), None, None),
        check_vma=False,
    )
```

```python
import math

import jax
import jax.numpy as jnp
from jax import lax
from jax.sharding import PartitionSpec as P

ITERS = 2


def padded_2(cells, sides, width):
    for axis, dim in sides:
        count = lax.axis_size(axis)
        ends = count - 1
        head = lax.slice_in_dim(cells, 0, width, axis=dim)
        tail = lax.slice_in_dim(cells, cells.shape[dim] - width, cells.shape[dim], axis=dim)
        cells = jnp.concatenate(
            [
                lax.ppermute(tail, axis, [(i, (i + 1) % count) for i in range(ends)]),
                cells,
                lax.ppermute(head, axis, [((i + 1) % count, i) for i in range(ends)]),
            ],
            axis=dim,
        )
    return cells


def gather_all(strip, axis):
    count = lax.axis_size(axis)
    copies = jnp.broadcast_to(strip[None], (count,) + strip.shape)
    joined = lax.all_to_all(copies, axis, 0, 0, tiled=True)
    return joined.reshape((count * strip.shape[0],) + strip.shape[1:])


def gather_rows(strip, axis):
    count = lax.axis_size(axis)
    bits = count.bit_length() - 1
    assert 1 << bits == count
    own = lax.axis_index(axis)
    joined = strip
    for depth, bit in enumerate(reversed(range(bits))):
        partner = lax.ppermute(joined, axis, [(i, i ^ (1 << bit)) for i in range(count)])
        upper = ((own >> bit) & 1) == 1
        low = jnp.where(upper, partner, joined)
        high = jnp.where(upper, joined, partner)
        joined = jnp.stack([low, high], axis=depth)
    return joined.reshape((count * strip.shape[0],) + strip.shape[1:])


def sum_rows(values, axis, levels=2):
    count = lax.axis_size(axis)
    own = lax.axis_index(axis)
    strip = values.shape[0] // count
    partial = values.reshape((count, strip) + values.shape[1:])
    for bit in range(levels):
        pairs = partial.reshape((partial.shape[0] // 2, 2) + partial.shape[1:])
        upper = ((own >> bit) & 1) == 1
        keep = jnp.where(upper, pairs[:, 1], pairs[:, 0])
        send = jnp.where(upper, pairs[:, 0], pairs[:, 1])
        moved = lax.ppermute(
            send.astype(jnp.bfloat16), axis, [(i, i ^ (1 << bit)) for i in range(count)]
        )
        partial = keep + moved.astype(jnp.float32)
    stride = 1 << levels
    groups = [list(range(r, count, stride)) for r in range(stride)]
    received = lax.all_to_all(
        partial.astype(jnp.bfloat16), axis, 0, 0, tiled=True, axis_index_groups=groups
    )
    return received.astype(jnp.float32).sum(axis=0)


def dft_tables(length):
    positions = jnp.arange(length, dtype=jnp.int32)
    angles = (positions[:, None] * positions[None, :] % length).astype(jnp.float32) * (
        2.0 * math.pi / length
    )
    norm_factor = 1.0 / math.sqrt(length)
    return (
        (jnp.cos(angles) * norm_factor).astype(jnp.bfloat16),
        (-jnp.sin(angles) * norm_factor).astype(jnp.bfloat16),
    )


def column_part(rounded, col_cat):
    row_count, source_count, col_count = rounded.shape
    product = jnp.dot(
        rounded.reshape(row_count * source_count, col_count),
        col_cat,
        preferred_element_type=jnp.float32,
    )
    return product.astype(jnp.bfloat16).reshape(row_count, source_count * 2 * col_count)


def combine_forward(real_prod, imag_prod, source_count, col_count):
    real_prod = real_prod.reshape(real_prod.shape[0], source_count, 2, col_count)
    imag_prod = imag_prod.reshape(imag_prod.shape[0], source_count, 2, col_count)
    real_out = real_prod[:, :, 0] - imag_prod[:, :, 1]
    imag_out = real_prod[:, :, 1] + imag_prod[:, :, 0]
    return jnp.stack([real_out, imag_out], axis=2)


def inverse_rows(row_real, row_imag, packed_grad, col_back, source_count, col_count):
    real_prod = jnp.dot(row_real, packed_grad, preferred_element_type=jnp.float32)
    imag_prod = jnp.dot(row_imag, packed_grad, preferred_element_type=jnp.float32)
    real_prod = real_prod.reshape(real_prod.shape[0], source_count, 2, col_count)
    imag_prod = imag_prod.reshape(imag_prod.shape[0], source_count, 2, col_count)
    real_out = real_prod[:, :, 0] + imag_prod[:, :, 1]
    imag_out = real_prod[:, :, 1] - imag_prod[:, :, 0]
    joined = jnp.concatenate([real_out, imag_out], axis=-1).astype(jnp.bfloat16)
    result = jnp.dot(
        joined.reshape(-1, 2 * col_count), col_back, preferred_element_type=jnp.float32
    )
    return result.reshape(real_prod.shape[0], source_count, col_count)


def block_gradient(fourier, data_block, beam_block, mix_block, level_block):
    predicted = jnp.einsum("ct,ktzl->kczl", mix_block, fourier)
    beam_gain = beam_block.astype(jnp.float32)[:, :, None, :]
    residual = data_block.astype(jnp.float32) - beam_gain * predicted
    weight = level_block.astype(jnp.float32) * 0.25
    weighted = weight[None, :, None, None] * beam_gain * residual
    summed = jnp.einsum("cs,kczl->kszl", mix_block, weighted)
    return summed.astype(jnp.bfloat16)


def smooth_rows(padded, spacing, row_count):
    return (
        padded[0:row_count]
        + 2.0 * padded[spacing : spacing + row_count]
        + padded[2 * spacing : 2 * spacing + row_count]
    ) * 0.25


def smooth_cols(values, spacing):
    padded = jnp.pad(values, ((0, 0), (0, 0), (spacing, spacing)))
    return (
        padded[..., : -2 * spacing]
        + 2.0 * padded[..., spacing:-spacing]
        + padded[..., 2 * spacing :]
    ) * 0.25


def shrink(values, bound_value):
    return values - jnp.clip(values, -bound_value, bound_value)


def combine_scales(updated, smooth_one, coarse, fine_bound, coarse_bound):
    return (
        coarse
        + shrink(smooth_one - coarse, coarse_bound)
        + shrink(updated - smooth_one, fine_bound)
    )


def body(sky_data, beam_gains, mixing, noise_levels, threshold_levels, start_sources):
    strip_rows, source_count, col_count = start_sources.shape
    full_rows = strip_rows * lax.axis_size("chan")
    row_real, row_imag = dft_tables(full_rows)
    col_real, col_imag = dft_tables(col_count)
    col_cat = jnp.concatenate([col_real, col_imag], axis=1)
    col_back = jnp.concatenate([col_real, col_imag], axis=0)
    bounds = threshold_levels.astype(jnp.float32) * 0.05
    fine_bound = bounds[:, 0][:, None]
    coarse_bound = bounds[:, 1][:, None]
    first_row = lax.axis_index("chan") * strip_rows
    sources = start_sources
    for iteration in range(ITERS):
        rounded = sources.astype(jnp.bfloat16)
        gather = gather_all if iteration == 0 else gather_rows
        gathered = gather(rounded, "chan")
        packed = column_part(gathered, col_cat)
        fourier = combine_forward(
            jnp.dot(row_real, packed, preferred_element_type=jnp.float32),
            jnp.dot(row_imag, packed, preferred_element_type=jnp.float32),
            source_count,
            col_count,
        )
        grad_local = block_gradient(fourier, sky_data, beam_gains, mixing, noise_levels)
        packed_grad = grad_local.reshape(full_rows, source_count * 2 * col_count)
        gradient = sum_rows(
            inverse_rows(row_real, row_imag, packed_grad, col_back, source_count, col_count),
            "chan",
        )
        updated = sources + gradient
        wide_pad = padded_2(updated, (("chan", 0),), 3)
        smooth_wide = smooth_cols(smooth_rows(wide_pad, 1, strip_rows + 4), 1)
        inside = (first_row - 2 + jnp.arange(strip_rows + 4) >= 0) & (
            first_row - 2 + jnp.arange(strip_rows + 4) < full_rows
        )
        smooth_wide = jnp.where(inside[:, None, None], smooth_wide, 0.0)
        smooth_one = smooth_wide[2 : 2 + strip_rows]
        coarse = smooth_cols(smooth_rows(smooth_wide, 2, strip_rows), 2)
        sources = combine_scales(updated, smooth_one, coarse, fine_bound, coarse_bound)
    return sources


def solution(mesh):
    return jax.shard_map(
        body,
        mesh=mesh,
        in_specs=(
            P("groups", "chan", None, None),
            P("groups", "chan", None),
            P(("groups", "chan"), None),
            P("chan"),
            P(),
            P(("groups", "chan"), None, None),
        ),
        out_specs=P(("groups", "chan"), None, None),
        check_vma=False,
    )
```

```python
import math

import jax
import jax.numpy as jnp
from jax import lax
from jax.sharding import PartitionSpec as P

ITERS = 2


def padded_2(cells, sides, width):
    for axis, dim in sides:
        count = lax.axis_size(axis)
        ends = count - 1
        head = lax.slice_in_dim(cells, 0, width, axis=dim)
        tail = lax.slice_in_dim(cells, cells.shape[dim] - width, cells.shape[dim], axis=dim)
        cells = jnp.concatenate(
            [
                lax.ppermute(tail, axis, [(i, (i + 1) % count) for i in range(ends)]),
                cells,
                lax.ppermute(head, axis, [((i + 1) % count, i) for i in range(ends)]),
            ],
            axis=dim,
        )
    return cells


def gather_all(strip, axis):
    count = lax.axis_size(axis)
    copies = jnp.broadcast_to(strip[None], (count,) + strip.shape)
    joined = lax.all_to_all(copies, axis, 0, 0, tiled=True)
    return joined.reshape((count * strip.shape[0],) + strip.shape[1:])


def gather_rows(strip, axis):
    count = lax.axis_size(axis)
    bits = count.bit_length() - 1
    assert 1 << bits == count
    own = lax.axis_index(axis)
    joined = strip
    for depth, bit in enumerate(reversed(range(bits))):
        partner = lax.ppermute(joined, axis, [(i, i ^ (1 << bit)) for i in range(count)])
        upper = ((own >> bit) & 1) == 1
        low = jnp.where(upper, partner, joined)
        high = jnp.where(upper, joined, partner)
        joined = jnp.stack([low, high], axis=depth)
    return joined.reshape((count * strip.shape[0],) + strip.shape[1:])


def sum_rows(values, axis):
    count = lax.axis_size(axis)
    half = count // 2
    parity = lax.axis_index(axis) % 2
    strip = values.shape[0] // count
    pairs = values.reshape((half, 2, strip) + values.shape[1:])
    even = pairs[:, 0]
    odd = pairs[:, 1]
    keep = jnp.where(parity == 1, odd, even)
    send = jnp.where(parity == 1, even, odd)
    moved = lax.ppermute(
        send.astype(jnp.bfloat16), axis, [(i, i ^ 1) for i in range(count)]
    )
    chip_sum = (keep + moved.astype(jnp.float32)).astype(jnp.bfloat16)
    groups = [list(range(p, count, 2)) for p in range(2)]
    received = lax.all_to_all(chip_sum, axis, 0, 0, tiled=True, axis_index_groups=groups)
    return received.astype(jnp.float32).sum(axis=0)


def dft_tables(length):
    positions = jnp.arange(length, dtype=jnp.int32)
    angles = (positions[:, None] * positions[None, :] % length).astype(jnp.float32) * (
        2.0 * math.pi / length
    )
    norm_factor = 1.0 / math.sqrt(length)
    return (
        (jnp.cos(angles) * norm_factor).astype(jnp.bfloat16),
        (-jnp.sin(angles) * norm_factor).astype(jnp.bfloat16),
    )


def column_part(rounded, col_cat):
    row_count, source_count, col_count = rounded.shape
    product = jnp.dot(
        rounded.reshape(row_count * source_count, col_count),
        col_cat,
        preferred_element_type=jnp.float32,
    )
    return product.astype(jnp.bfloat16).reshape(row_count, source_count * 2 * col_count)


def combine_forward(real_prod, imag_prod, source_count, col_count):
    real_prod = real_prod.reshape(real_prod.shape[0], source_count, 2, col_count)
    imag_prod = imag_prod.reshape(imag_prod.shape[0], source_count, 2, col_count)
    real_out = real_prod[:, :, 0] - imag_prod[:, :, 1]
    imag_out = real_prod[:, :, 1] + imag_prod[:, :, 0]
    return jnp.stack([real_out, imag_out], axis=2)


def inverse_rows(row_real, row_imag, packed_grad, col_back, source_count, col_count):
    real_prod = jnp.dot(row_real, packed_grad, preferred_element_type=jnp.float32)
    imag_prod = jnp.dot(row_imag, packed_grad, preferred_element_type=jnp.float32)
    real_prod = real_prod.reshape(real_prod.shape[0], source_count, 2, col_count)
    imag_prod = imag_prod.reshape(imag_prod.shape[0], source_count, 2, col_count)
    real_out = real_prod[:, :, 0] + imag_prod[:, :, 1]
    imag_out = real_prod[:, :, 1] - imag_prod[:, :, 0]
    joined = jnp.concatenate([real_out, imag_out], axis=-1).astype(jnp.bfloat16)
    result = jnp.dot(
        joined.reshape(-1, 2 * col_count), col_back, preferred_element_type=jnp.float32
    )
    return result.reshape(real_prod.shape[0], source_count, col_count)


def block_gradient(fourier, data_block, beam_block, mix_block, level_block):
    predicted = jnp.einsum("ct,ktzl->kczl", mix_block, fourier)
    beam_gain = beam_block.astype(jnp.float32)[:, :, None, :]
    residual = data_block.astype(jnp.float32) - beam_gain * predicted
    weight = level_block.astype(jnp.float32) * 0.25
    weighted_mix = mix_block * weight[:, None]
    summed = jnp.einsum("cs,kczl->kszl", weighted_mix, beam_gain * residual)
    return summed.astype(jnp.bfloat16)


def smooth_rows(padded, spacing, row_count):
    return (
        padded[0:row_count]
        + 2.0 * padded[spacing : spacing + row_count]
        + padded[2 * spacing : 2 * spacing + row_count]
    ) * 0.25


def smooth_cols(values, spacing):
    padded = jnp.pad(values, ((0, 0), (0, 0), (spacing, spacing)))
    return (
        padded[..., : -2 * spacing]
        + 2.0 * padded[..., spacing:-spacing]
        + padded[..., 2 * spacing :]
    ) * 0.25


def shrink(values, bound_value):
    return values - jnp.clip(values, -bound_value, bound_value)


def combine_scales(updated, smooth_one, coarse, fine_bound, coarse_bound):
    return (
        coarse
        + shrink(smooth_one - coarse, coarse_bound)
        + shrink(updated - smooth_one, fine_bound)
    )


def body(sky_data, beam_gains, mixing, noise_levels, threshold_levels, start_sources):
    strip_rows, source_count, col_count = start_sources.shape
    full_rows = strip_rows * lax.axis_size("chan")
    row_real, row_imag = dft_tables(full_rows)
    col_real, col_imag = dft_tables(col_count)
    col_cat = jnp.concatenate([col_real, col_imag], axis=1)
    col_back = jnp.concatenate([col_real, col_imag], axis=0)
    bounds = threshold_levels.astype(jnp.float32) * 0.05
    fine_bound = bounds[:, 0][:, None]
    coarse_bound = bounds[:, 1][:, None]
    first_row = lax.axis_index("chan") * strip_rows
    sources = start_sources
    for iteration in range(ITERS):
        rounded = sources.astype(jnp.bfloat16)
        gather = gather_all if iteration == 0 else gather_rows
        gathered = gather(rounded, "chan")
        packed = column_part(gathered, col_cat)
        fourier = combine_forward(
            jnp.dot(row_real, packed, preferred_element_type=jnp.float32),
            jnp.dot(row_imag, packed, preferred_element_type=jnp.float32),
            source_count,
            col_count,
        )
        grad_local = block_gradient(fourier, sky_data, beam_gains, mixing, noise_levels)
        packed_grad = grad_local.reshape(full_rows, source_count * 2 * col_count)
        gradient = sum_rows(
            inverse_rows(row_real, row_imag, packed_grad, col_back, source_count, col_count),
            "chan",
        )
        updated = sources + gradient
        wide_pad = padded_2(updated, (("chan", 0),), 3)
        smooth_wide = smooth_cols(smooth_rows(wide_pad, 1, strip_rows + 4), 1)
        inside = (first_row - 2 + jnp.arange(strip_rows + 4) >= 0) & (
            first_row - 2 + jnp.arange(strip_rows + 4) < full_rows
        )
        smooth_wide = jnp.where(inside[:, None, None], smooth_wide, 0.0)
        smooth_one = smooth_wide[2 : 2 + strip_rows]
        coarse = smooth_cols(smooth_rows(smooth_wide, 2, strip_rows), 2)
        sources = combine_scales(updated, smooth_one, coarse, fine_bound, coarse_bound)
    return sources


def solution(mesh):
    return jax.shard_map(
        body,
        mesh=mesh,
        in_specs=(
            P("groups", "chan", None, None),
            P("groups", "chan", None),
            P(("groups", "chan"), None),
            P("chan"),
            P(),
            P(("groups", "chan"), None, None),
        ),
        out_specs=P(("groups", "chan"), None, None),
        check_vma=False,
    )
```

```python
import math

import jax
import jax.numpy as jnp
from jax import lax
from jax.sharding import PartitionSpec as P

ITERS = 2


def padded_2(cells, sides, width):
    for axis, dim in sides:
        count = lax.axis_size(axis)
        ends = count - 1
        head = lax.slice_in_dim(cells, 0, width, axis=dim)
        tail = lax.slice_in_dim(cells, cells.shape[dim] - width, cells.shape[dim], axis=dim)
        cells = jnp.concatenate(
            [
                lax.ppermute(tail, axis, [(i, (i + 1) % count) for i in range(ends)]),
                cells,
                lax.ppermute(head, axis, [((i + 1) % count, i) for i in range(ends)]),
            ],
            axis=dim,
        )
    return cells


def gather_all(strip, axis):
    count = lax.axis_size(axis)
    copies = jnp.broadcast_to(strip[None], (count,) + strip.shape)
    joined = lax.all_to_all(copies, axis, 0, 0, tiled=True)
    return joined.reshape((count * strip.shape[0],) + strip.shape[1:])


def gather_rows(strip, axis):
    count = lax.axis_size(axis)
    bits = count.bit_length() - 1
    assert 1 << bits == count
    own = lax.axis_index(axis)
    joined = strip
    for depth, bit in enumerate(reversed(range(bits))):
        partner = lax.ppermute(joined, axis, [(i, i ^ (1 << bit)) for i in range(count)])
        upper = ((own >> bit) & 1) == 1
        low = jnp.where(upper, partner, joined)
        high = jnp.where(upper, joined, partner)
        joined = jnp.stack([low, high], axis=depth)
    return joined.reshape((count * strip.shape[0],) + strip.shape[1:])


def sum_rows(values, axis):
    count = lax.axis_size(axis)
    half = count // 2
    parity = lax.axis_index(axis) % 2
    strip = values.shape[0] // count
    pairs = values.reshape((half, 2, strip) + values.shape[1:])
    even = pairs[:, 0]
    odd = pairs[:, 1]
    keep = jnp.where(parity == 1, odd, even)
    send = jnp.where(parity == 1, even, odd)
    moved = lax.ppermute(
        send.astype(jnp.bfloat16), axis, [(i, i ^ 1) for i in range(count)]
    )
    chip_sum = (keep + moved.astype(jnp.float32)).astype(jnp.bfloat16)
    groups = [list(range(p, count, 2)) for p in range(2)]
    received = lax.all_to_all(chip_sum, axis, 0, 0, tiled=True, axis_index_groups=groups)
    return received.astype(jnp.float32).sum(axis=0)


def dft_tables(length):
    positions = jnp.arange(length, dtype=jnp.int32)
    angles = (positions[:, None] * positions[None, :] % length).astype(jnp.float32) * (
        2.0 * math.pi / length
    )
    norm_factor = 1.0 / math.sqrt(length)
    return (
        (jnp.cos(angles) * norm_factor).astype(jnp.bfloat16),
        (-jnp.sin(angles) * norm_factor).astype(jnp.bfloat16),
    )


def column_part(rounded, col_cat):
    row_count, source_count, col_count = rounded.shape
    product = jnp.dot(
        rounded.reshape(row_count * source_count, col_count),
        col_cat,
        preferred_element_type=jnp.float32,
    )
    return product.astype(jnp.bfloat16).reshape(row_count, source_count * 2 * col_count)


def combine_forward(real_prod, imag_prod, source_count, col_count):
    real_prod = real_prod.reshape(real_prod.shape[0], source_count, 2, col_count)
    imag_prod = imag_prod.reshape(imag_prod.shape[0], source_count, 2, col_count)
    real_out = real_prod[:, :, 0] - imag_prod[:, :, 1]
    imag_out = real_prod[:, :, 1] + imag_prod[:, :, 0]
    return jnp.stack([real_out, imag_out], axis=2)


def inverse_rows(row_both, packed_grad, col_back, source_count, col_count):
    both = jnp.dot(row_both, packed_grad, preferred_element_type=jnp.float32)
    real_prod = both[: row_both.shape[0] // 2]
    imag_prod = both[row_both.shape[0] // 2 :]
    real_prod = real_prod.reshape(real_prod.shape[0], source_count, 2, col_count)
    imag_prod = imag_prod.reshape(imag_prod.shape[0], source_count, 2, col_count)
    real_out = real_prod[:, :, 0] + imag_prod[:, :, 1]
    imag_out = real_prod[:, :, 1] - imag_prod[:, :, 0]
    joined = jnp.concatenate([real_out, imag_out], axis=-1).astype(jnp.bfloat16)
    result = jnp.dot(
        joined.reshape(-1, 2 * col_count), col_back, preferred_element_type=jnp.float32
    )
    return result.reshape(real_prod.shape[0], source_count, col_count)


def block_gradient(fourier, data_block, beam_block, mix_block, level_block):
    predicted = jnp.einsum("ct,ktzl->kczl", mix_block, fourier)
    beam_gain = beam_block.astype(jnp.float32)[:, :, None, :]
    residual = data_block.astype(jnp.float32) - beam_gain * predicted
    weight = level_block.astype(jnp.float32) * 0.25
    weighted_mix = mix_block * weight[:, None]
    summed = jnp.einsum("cs,kczl->kszl", weighted_mix, beam_gain * residual)
    return summed.astype(jnp.bfloat16)


def smooth_rows(padded, spacing, row_count):
    return (
        padded[0:row_count]
        + 2.0 * padded[spacing : spacing + row_count]
        + padded[2 * spacing : 2 * spacing + row_count]
    ) * 0.25


def smooth_cols(values, spacing):
    padded = jnp.pad(values, ((0, 0), (0, 0), (spacing, spacing)))
    return (
        padded[..., : -2 * spacing]
        + 2.0 * padded[..., spacing:-spacing]
        + padded[..., 2 * spacing :]
    ) * 0.25


def shrink(values, bound_value):
    return values - jnp.clip(values, -bound_value, bound_value)


def combine_scales(updated, smooth_one, coarse, fine_bound, coarse_bound):
    return (
        coarse
        + shrink(smooth_one - coarse, coarse_bound)
        + shrink(updated - smooth_one, fine_bound)
    )


def body(sky_data, beam_gains, mixing, noise_levels, threshold_levels, start_sources):
    strip_rows, source_count, col_count = start_sources.shape
    full_rows = strip_rows * lax.axis_size("chan")
    row_real, row_imag = dft_tables(full_rows)
    col_real, col_imag = dft_tables(col_count)
    row_both = jnp.concatenate([row_real, row_imag], axis=0)
    col_cat = jnp.concatenate([col_real, col_imag], axis=1)
    col_back = jnp.concatenate([col_real, col_imag], axis=0)
    bounds = threshold_levels.astype(jnp.float32) * 0.05
    fine_bound = bounds[:, 0][:, None]
    coarse_bound = bounds[:, 1][:, None]
    first_row = lax.axis_index("chan") * strip_rows
    sources = start_sources
    for iteration in range(ITERS):
        rounded = sources.astype(jnp.bfloat16)
        gather = gather_all if iteration == 0 else gather_rows
        gathered = gather(rounded, "chan")
        packed = column_part(gathered, col_cat)
        both = jnp.dot(row_both, packed, preferred_element_type=jnp.float32)
        fourier = combine_forward(both[:full_rows], both[full_rows:], source_count, col_count)
        grad_local = block_gradient(fourier, sky_data, beam_gains, mixing, noise_levels)
        packed_grad = grad_local.reshape(full_rows, source_count * 2 * col_count)
        gradient = sum_rows(
            inverse_rows(row_both, packed_grad, col_back, source_count, col_count),
            "chan",
        )
        updated = sources + gradient
        wide_pad = padded_2(updated, (("chan", 0),), 3)
        smooth_wide = smooth_cols(smooth_rows(wide_pad, 1, strip_rows + 4), 1)
        inside = (first_row - 2 + jnp.arange(strip_rows + 4) >= 0) & (
            first_row - 2 + jnp.arange(strip_rows + 4) < full_rows
        )
        smooth_wide = jnp.where(inside[:, None, None], smooth_wide, 0.0)
        smooth_one = smooth_wide[2 : 2 + strip_rows]
        coarse = smooth_cols(smooth_rows(smooth_wide, 2, strip_rows), 2)
        sources = combine_scales(updated, smooth_one, coarse, fine_bound, coarse_bound)
    return sources


def solution(mesh):
    return jax.shard_map(
        body,
        mesh=mesh,
        in_specs=(
            P("groups", "chan", None, None),
            P("groups", "chan", None),
            P(("groups", "chan"), None),
            P("chan"),
            P(),
            P(("groups", "chan"), None, None),
        ),
        out_specs=P(("groups", "chan"), None, None),
        check_vma=False,
    )
```

```python
import math

import jax
import jax.numpy as jnp
from jax import lax
from jax.sharding import PartitionSpec as P

ITERS = 2


def padded_2(cells, sides, width):
    for axis, dim in sides:
        count = lax.axis_size(axis)
        ends = count - 1
        head = lax.slice_in_dim(cells, 0, width, axis=dim)
        tail = lax.slice_in_dim(cells, cells.shape[dim] - width, cells.shape[dim], axis=dim)
        cells = jnp.concatenate(
            [
                lax.ppermute(tail, axis, [(i, (i + 1) % count) for i in range(ends)]),
                cells,
                lax.ppermute(head, axis, [((i + 1) % count, i) for i in range(ends)]),
            ],
            axis=dim,
        )
    return cells


def gather_all(strip, axis):
    count = lax.axis_size(axis)
    copies = jnp.broadcast_to(strip[None], (count,) + strip.shape)
    joined = lax.all_to_all(copies, axis, 0, 0, tiled=True)
    return joined.reshape((count * strip.shape[0],) + strip.shape[1:])


def gather_rows(strip, axis):
    count = lax.axis_size(axis)
    bits = count.bit_length() - 1
    assert 1 << bits == count
    own = lax.axis_index(axis)
    joined = strip
    for depth, bit in enumerate(reversed(range(bits))):
        partner = lax.ppermute(joined, axis, [(i, i ^ (1 << bit)) for i in range(count)])
        upper = ((own >> bit) & 1) == 1
        low = jnp.where(upper, partner, joined)
        high = jnp.where(upper, joined, partner)
        joined = jnp.stack([low, high], axis=depth)
    return joined.reshape((count * strip.shape[0],) + strip.shape[1:])


def sum_rows(values, axis):
    count = lax.axis_size(axis)
    half = count // 2
    parity = lax.axis_index(axis) % 2
    strip = values.shape[0] // count
    pairs = values.reshape((half, 2, strip) + values.shape[1:])
    even = pairs[:, 0]
    odd = pairs[:, 1]
    keep = jnp.where(parity == 1, odd, even)
    send = jnp.where(parity == 1, even, odd)
    moved = lax.ppermute(
        send.astype(jnp.bfloat16), axis, [(i, i ^ 1) for i in range(count)]
    )
    chip_sum = (keep + moved.astype(jnp.float32)).astype(jnp.bfloat16)
    groups = [list(range(p, count, 2)) for p in range(2)]
    received = lax.all_to_all(chip_sum, axis, 0, 0, tiled=True, axis_index_groups=groups)
    return received.astype(jnp.float32).sum(axis=0)


def dft_tables(length):
    positions = jnp.arange(length, dtype=jnp.int32)
    angles = (positions[:, None] * positions[None, :] % length).astype(jnp.float32) * (
        2.0 * math.pi / length
    )
    norm_factor = 1.0 / math.sqrt(length)
    return (
        (jnp.cos(angles) * norm_factor).astype(jnp.bfloat16),
        (-jnp.sin(angles) * norm_factor).astype(jnp.bfloat16),
    )


def column_part(rounded, col_cat):
    row_count, source_count, col_count = rounded.shape
    product = jnp.dot(
        rounded.reshape(row_count * source_count, col_count),
        col_cat,
        preferred_element_type=jnp.float32,
    )
    return product.astype(jnp.bfloat16).reshape(row_count, source_count * 2 * col_count)


def combine_forward(real_prod, imag_prod, source_count, col_count):
    real_prod = real_prod.reshape(real_prod.shape[0], source_count, 2, col_count)
    imag_prod = imag_prod.reshape(imag_prod.shape[0], source_count, 2, col_count)
    real_out = real_prod[:, :, 0] - imag_prod[:, :, 1]
    imag_out = real_prod[:, :, 1] + imag_prod[:, :, 0]
    return jnp.stack([real_out, imag_out], axis=2)


def forward_part(gathered, row_real, row_imag, col_cat):
    packed = column_part(gathered, col_cat)
    return combine_forward(
        jnp.dot(row_real, packed, preferred_element_type=jnp.float32),
        jnp.dot(row_imag, packed, preferred_element_type=jnp.float32),
        gathered.shape[1],
        gathered.shape[2],
    )


def inverse_rows(row_real, row_imag, packed_grad, col_back, source_count, col_count):
    real_prod = jnp.dot(row_real, packed_grad, preferred_element_type=jnp.float32)
    imag_prod = jnp.dot(row_imag, packed_grad, preferred_element_type=jnp.float32)
    real_prod = real_prod.reshape(real_prod.shape[0], source_count, 2, col_count)
    imag_prod = imag_prod.reshape(imag_prod.shape[0], source_count, 2, col_count)
    real_out = real_prod[:, :, 0] + imag_prod[:, :, 1]
    imag_out = real_prod[:, :, 1] - imag_prod[:, :, 0]
    joined = jnp.concatenate([real_out, imag_out], axis=-1).astype(jnp.bfloat16)
    result = jnp.dot(
        joined.reshape(-1, 2 * col_count), col_back, preferred_element_type=jnp.float32
    )
    return result.reshape(real_prod.shape[0], source_count, col_count)


def block_gradient(fourier, data_block, beam_block, mix_block, level_block):
    predicted = jnp.einsum("ct,ktzl->kczl", mix_block, fourier)
    beam_gain = beam_block.astype(jnp.float32)[:, :, None, :]
    residual = data_block.astype(jnp.float32) - beam_gain * predicted
    weight = level_block.astype(jnp.float32) * 0.25
    weighted_mix = mix_block * weight[:, None]
    summed = jnp.einsum("cs,kczl->kszl", weighted_mix, beam_gain * residual)
    return summed.astype(jnp.bfloat16)


def smooth_rows(padded, spacing, row_count):
    return (
        padded[0:row_count]
        + 2.0 * padded[spacing : spacing + row_count]
        + padded[2 * spacing : 2 * spacing + row_count]
    ) * 0.25


def smooth_cols(values, spacing):
    padded = jnp.pad(values, ((0, 0), (0, 0), (spacing, spacing)))
    return (
        padded[..., : -2 * spacing]
        + 2.0 * padded[..., spacing:-spacing]
        + padded[..., 2 * spacing :]
    ) * 0.25


def shrink(values, bound_value):
    return values - jnp.clip(values, -bound_value, bound_value)


def combine_scales(updated, smooth_one, coarse, fine_bound, coarse_bound):
    return (
        coarse
        + shrink(smooth_one - coarse, coarse_bound)
        + shrink(updated - smooth_one, fine_bound)
    )


def body(sky_data, beam_gains, mixing, noise_levels, threshold_levels, start_sources):
    strip_rows, source_count, col_count = start_sources.shape
    full_rows = strip_rows * lax.axis_size("chan")
    row_real, row_imag = dft_tables(full_rows)
    col_real, col_imag = dft_tables(col_count)
    col_cat = jnp.concatenate([col_real, col_imag], axis=1)
    col_back = jnp.concatenate([col_real, col_imag], axis=0)
    bounds = threshold_levels.astype(jnp.float32) * 0.05
    fine_bound = bounds[:, 0][:, None]
    coarse_bound = bounds[:, 1][:, None]
    first_row = lax.axis_index("chan") * strip_rows
    sources = start_sources
    for iteration in range(ITERS):
        rounded = sources.astype(jnp.bfloat16)
        if iteration == 0:
            parts = [rounded[:, : source_count // 2], rounded[:, source_count // 2 :]]
            parts = [gather_all(part, "chan") for part in parts]
        else:
            parts = [gather_rows(rounded, "chan")]
        fourier = jnp.concatenate(
            [forward_part(part, row_real, row_imag, col_cat) for part in parts], axis=1
        )
        grad_local = block_gradient(fourier, sky_data, beam_gains, mixing, noise_levels)
        packed_grad = grad_local.reshape(full_rows, source_count * 2 * col_count)
        gradient = sum_rows(
            inverse_rows(row_real, row_imag, packed_grad, col_back, source_count, col_count),
            "chan",
        )
        updated = sources + gradient
        wide_pad = padded_2(updated, (("chan", 0),), 3)
        smooth_wide = smooth_cols(smooth_rows(wide_pad, 1, strip_rows + 4), 1)
        inside = (first_row - 2 + jnp.arange(strip_rows + 4) >= 0) & (
            first_row - 2 + jnp.arange(strip_rows + 4) < full_rows
        )
        smooth_wide = jnp.where(inside[:, None, None], smooth_wide, 0.0)
        smooth_one = smooth_wide[2 : 2 + strip_rows]
        coarse = smooth_cols(smooth_rows(smooth_wide, 2, strip_rows), 2)
        sources = combine_scales(updated, smooth_one, coarse, fine_bound, coarse_bound)
    return sources


def solution(mesh):
    return jax.shard_map(
        body,
        mesh=mesh,
        in_specs=(
            P("groups", "chan", None, None),
            P("groups", "chan", None),
            P(("groups", "chan"), None),
            P("chan"),
            P(),
            P(("groups", "chan"), None, None),
        ),
        out_specs=P(("groups", "chan"), None, None),
        check_vma=False,
    )
```

```python
import math

import jax
import jax.numpy as jnp
from jax import lax
from jax.sharding import PartitionSpec as P

ITERS = 2


def padded_2(cells, sides, width):
    for axis, dim in sides:
        count = lax.axis_size(axis)
        ends = count - 1
        head = lax.slice_in_dim(cells, 0, width, axis=dim)
        tail = lax.slice_in_dim(cells, cells.shape[dim] - width, cells.shape[dim], axis=dim)
        cells = jnp.concatenate(
            [
                lax.ppermute(tail, axis, [(i, (i + 1) % count) for i in range(ends)]),
                cells,
                lax.ppermute(head, axis, [((i + 1) % count, i) for i in range(ends)]),
            ],
            axis=dim,
        )
    return cells


def gather_all(strip, axis):
    count = lax.axis_size(axis)
    copies = jnp.broadcast_to(strip[None], (count,) + strip.shape)
    joined = lax.all_to_all(copies, axis, 0, 0, tiled=True)
    return joined.reshape((count * strip.shape[0],) + strip.shape[1:])


def gather_rows(strip, axis):
    count = lax.axis_size(axis)
    bits = count.bit_length() - 1
    assert 1 << bits == count
    own = lax.axis_index(axis)
    order = [1] + list(reversed(range(2, bits))) + [0] if bits > 2 else list(reversed(range(bits)))
    joined = strip[(None,) * bits]
    for bit in order:
        partner = lax.ppermute(joined, axis, [(i, i ^ (1 << bit)) for i in range(count)])
        upper = ((own >> bit) & 1) == 1
        low = jnp.where(upper, partner, joined)
        high = jnp.where(upper, joined, partner)
        joined = jnp.concatenate([low, high], axis=bits - 1 - bit)
    return joined.reshape((count * strip.shape[0],) + strip.shape[1:])


def sum_rows(values, axis):
    count = lax.axis_size(axis)
    half = count // 2
    parity = lax.axis_index(axis) % 2
    strip = values.shape[0] // count
    pairs = values.reshape((half, 2, strip) + values.shape[1:])
    even = pairs[:, 0]
    odd = pairs[:, 1]
    keep = jnp.where(parity == 1, odd, even)
    send = jnp.where(parity == 1, even, odd)
    moved = lax.ppermute(
        send.astype(jnp.bfloat16), axis, [(i, i ^ 1) for i in range(count)]
    )
    chip_sum = (keep + moved.astype(jnp.float32)).astype(jnp.bfloat16)
    groups = [list(range(p, count, 2)) for p in range(2)]
    received = lax.all_to_all(chip_sum, axis, 0, 0, tiled=True, axis_index_groups=groups)
    return received.astype(jnp.float32).sum(axis=0)


def dft_tables(length):
    positions = jnp.arange(length, dtype=jnp.int32)
    angles = (positions[:, None] * positions[None, :] % length).astype(jnp.float32) * (
        2.0 * math.pi / length
    )
    norm_factor = 1.0 / math.sqrt(length)
    return (
        (jnp.cos(angles) * norm_factor).astype(jnp.bfloat16),
        (-jnp.sin(angles) * norm_factor).astype(jnp.bfloat16),
    )


def column_part(rounded, col_cat):
    row_count, source_count, col_count = rounded.shape
    product = jnp.dot(
        rounded.reshape(row_count * source_count, col_count),
        col_cat,
        preferred_element_type=jnp.float32,
    )
    return product.astype(jnp.bfloat16).reshape(row_count, source_count * 2 * col_count)


def combine_forward(real_prod, imag_prod, source_count, col_count):
    real_prod = real_prod.reshape(real_prod.shape[0], source_count, 2, col_count)
    imag_prod = imag_prod.reshape(imag_prod.shape[0], source_count, 2, col_count)
    real_out = real_prod[:, :, 0] - imag_prod[:, :, 1]
    imag_out = real_prod[:, :, 1] + imag_prod[:, :, 0]
    return jnp.stack([real_out, imag_out], axis=2)


def inverse_rows(row_real, row_imag, packed_grad, col_back, source_count, col_count):
    real_prod = jnp.dot(row_real, packed_grad, preferred_element_type=jnp.float32)
    imag_prod = jnp.dot(row_imag, packed_grad, preferred_element_type=jnp.float32)
    real_prod = real_prod.reshape(real_prod.shape[0], source_count, 2, col_count)
    imag_prod = imag_prod.reshape(imag_prod.shape[0], source_count, 2, col_count)
    real_out = real_prod[:, :, 0] + imag_prod[:, :, 1]
    imag_out = real_prod[:, :, 1] - imag_prod[:, :, 0]
    joined = jnp.concatenate([real_out, imag_out], axis=-1).astype(jnp.bfloat16)
    result = jnp.dot(
        joined.reshape(-1, 2 * col_count), col_back, preferred_element_type=jnp.float32
    )
    return result.reshape(real_prod.shape[0], source_count, col_count)


def block_gradient(fourier, data_block, beam_block, mix_block, level_block):
    predicted = jnp.einsum("ct,ktzl->kczl", mix_block, fourier)
    beam_gain = beam_block.astype(jnp.float32)[:, :, None, :]
    residual = data_block.astype(jnp.float32) - beam_gain * predicted
    weight = level_block.astype(jnp.float32) * 0.25
    weighted_mix = mix_block * weight[:, None]
    summed = jnp.einsum("cs,kczl->kszl", weighted_mix, beam_gain * residual)
    return summed.astype(jnp.bfloat16)


def smooth_rows(padded, spacing, row_count):
    return (
        padded[0:row_count]
        + 2.0 * padded[spacing : spacing + row_count]
        + padded[2 * spacing : 2 * spacing + row_count]
    ) * 0.25


def smooth_cols(values, spacing):
    padded = jnp.pad(values, ((0, 0), (0, 0), (spacing, spacing)))
    return (
        padded[..., : -2 * spacing]
        + 2.0 * padded[..., spacing:-spacing]
        + padded[..., 2 * spacing :]
    ) * 0.25


def shrink(values, bound_value):
    return values - jnp.clip(values, -bound_value, bound_value)


def combine_scales(updated, smooth_one, coarse, fine_bound, coarse_bound):
    return (
        coarse
        + shrink(smooth_one - coarse, coarse_bound)
        + shrink(updated - smooth_one, fine_bound)
    )


def body(sky_data, beam_gains, mixing, noise_levels, threshold_levels, start_sources):
    strip_rows, source_count, col_count = start_sources.shape
    full_rows = strip_rows * lax.axis_size("chan")
    row_real, row_imag = dft_tables(full_rows)
    col_real, col_imag = dft_tables(col_count)
    col_cat = jnp.concatenate([col_real, col_imag], axis=1)
    col_back = jnp.concatenate([col_real, col_imag], axis=0)
    bounds = threshold_levels.astype(jnp.float32) * 0.05
    fine_bound = bounds[:, 0][:, None]
    coarse_bound = bounds[:, 1][:, None]
    first_row = lax.axis_index("chan") * strip_rows
    sources = start_sources
    for iteration in range(ITERS):
        rounded = sources.astype(jnp.bfloat16)
        gather = gather_all if iteration == 0 else gather_rows
        gathered = gather(rounded, "chan")
        packed = column_part(gathered, col_cat)
        fourier = combine_forward(
            jnp.dot(row_real, packed, preferred_element_type=jnp.float32),
            jnp.dot(row_imag, packed, preferred_element_type=jnp.float32),
            source_count,
            col_count,
        )
        grad_local = block_gradient(fourier, sky_data, beam_gains, mixing, noise_levels)
        packed_grad = grad_local.reshape(full_rows, source_count * 2 * col_count)
        gradient = sum_rows(
            inverse_rows(row_real, row_imag, packed_grad, col_back, source_count, col_count),
            "chan",
        )
        updated = sources + gradient
        wide_pad = padded_2(updated, (("chan", 0),), 3)
        smooth_wide = smooth_cols(smooth_rows(wide_pad, 1, strip_rows + 4), 1)
        inside = (first_row - 2 + jnp.arange(strip_rows + 4) >= 0) & (
            first_row - 2 + jnp.arange(strip_rows + 4) < full_rows
        )
        smooth_wide = jnp.where(inside[:, None, None], smooth_wide, 0.0)
        smooth_one = smooth_wide[2 : 2 + strip_rows]
        coarse = smooth_cols(smooth_rows(smooth_wide, 2, strip_rows), 2)
        sources = combine_scales(updated, smooth_one, coarse, fine_bound, coarse_bound)
    return sources


def solution(mesh):
    return jax.shard_map(
        body,
        mesh=mesh,
        in_specs=(
            P("groups", "chan", None, None),
            P("groups", "chan", None),
            P(("groups", "chan"), None),
            P("chan"),
            P(),
            P(("groups", "chan"), None, None),
        ),
        out_specs=P(("groups", "chan"), None, None),
        check_vma=False,
    )
```

```python
import math

import jax
import jax.numpy as jnp
from jax import lax
from jax.sharding import PartitionSpec as P

ITERS = 2


def padded_2(cells, sides, width):
    for axis, dim in sides:
        count = lax.axis_size(axis)
        ends = count - 1
        head = lax.slice_in_dim(cells, 0, width, axis=dim)
        tail = lax.slice_in_dim(cells, cells.shape[dim] - width, cells.shape[dim], axis=dim)
        cells = jnp.concatenate(
            [
                lax.ppermute(tail, axis, [(i, (i + 1) % count) for i in range(ends)]),
                cells,
                lax.ppermute(head, axis, [((i + 1) % count, i) for i in range(ends)]),
            ],
            axis=dim,
        )
    return cells


def gather_all(strip, axis):
    count = lax.axis_size(axis)
    copies = jnp.broadcast_to(strip[None], (count,) + strip.shape)
    joined = lax.all_to_all(copies, axis, 0, 0, tiled=True)
    return joined.reshape((count * strip.shape[0],) + strip.shape[1:])


def gather_rows(strip, axis):
    count = lax.axis_size(axis)
    bits = count.bit_length() - 1
    assert 1 << bits == count
    own = lax.axis_index(axis)
    joined = strip
    for depth, bit in enumerate(reversed(range(bits))):
        partner = lax.ppermute(joined, axis, [(i, i ^ (1 << bit)) for i in range(count)])
        upper = ((own >> bit) & 1) == 1
        low = jnp.where(upper, partner, joined)
        high = jnp.where(upper, joined, partner)
        joined = jnp.stack([low, high], axis=depth)
    return joined.reshape((count * strip.shape[0],) + strip.shape[1:])


def sum_rows(values, axis):
    count = lax.axis_size(axis)
    half = count // 2
    parity = lax.axis_index(axis) % 2
    strip = values.shape[0] // count
    pairs = values.reshape((half, 2, strip) + values.shape[1:])
    even = pairs[:, 0]
    odd = pairs[:, 1]
    keep = jnp.where(parity == 1, odd, even)
    send = jnp.where(parity == 1, even, odd)
    moved = lax.ppermute(
        send.astype(jnp.bfloat16), axis, [(i, i ^ 1) for i in range(count)]
    )
    chip_sum = (keep + moved.astype(jnp.float32)).astype(jnp.bfloat16)
    groups = [list(range(p, count, 2)) for p in range(2)]
    received = lax.all_to_all(chip_sum, axis, 0, 0, tiled=True, axis_index_groups=groups)
    return received.astype(jnp.float32).sum(axis=0)


def dft_tables(length):
    positions = jnp.arange(length, dtype=jnp.int32)
    angles = (positions[:, None] * positions[None, :] % length).astype(jnp.float32) * (
        2.0 * math.pi / length
    )
    norm_factor = 1.0 / math.sqrt(length)
    return (
        (jnp.cos(angles) * norm_factor).astype(jnp.bfloat16),
        (-jnp.sin(angles) * norm_factor).astype(jnp.bfloat16),
    )


def column_part(rounded, col_cat):
    row_count, source_count, col_count = rounded.shape
    product = jnp.dot(
        rounded.reshape(row_count * source_count, col_count),
        col_cat,
        preferred_element_type=jnp.float32,
    )
    return product.astype(jnp.bfloat16).reshape(row_count, source_count * 2 * col_count)


def combine_forward(real_prod, imag_prod, source_count, col_count):
    real_prod = real_prod.reshape(real_prod.shape[0], source_count, 2, col_count)
    imag_prod = imag_prod.reshape(imag_prod.shape[0], source_count, 2, col_count)
    real_out = real_prod[:, :, 0] - imag_prod[:, :, 1]
    imag_out = real_prod[:, :, 1] + imag_prod[:, :, 0]
    return jnp.stack([real_out, imag_out], axis=2)


def inverse_rows(row_real, row_imag, packed_grad, col_back, source_count, col_count):
    real_prod = jnp.dot(row_real, packed_grad, preferred_element_type=jnp.float32)
    imag_prod = jnp.dot(row_imag, packed_grad, preferred_element_type=jnp.float32)
    real_prod = real_prod.reshape(real_prod.shape[0], source_count, 2, col_count)
    imag_prod = imag_prod.reshape(imag_prod.shape[0], source_count, 2, col_count)
    real_out = real_prod[:, :, 0] + imag_prod[:, :, 1]
    imag_out = real_prod[:, :, 1] - imag_prod[:, :, 0]
    joined = jnp.concatenate([real_out, imag_out], axis=-1).astype(jnp.bfloat16)
    result = jnp.dot(
        joined.reshape(-1, 2 * col_count), col_back, preferred_element_type=jnp.float32
    )
    return result.reshape(real_prod.shape[0], source_count, col_count)


def block_gradient(fourier, data_block, beam_block, mix_block, level_block):
    predicted = jnp.einsum("ct,ktzl->kczl", mix_block, fourier)
    beam_gain = beam_block.astype(jnp.float32)[:, :, None, :]
    residual = data_block.astype(jnp.float32) - beam_gain * predicted
    weight = level_block.astype(jnp.float32) * 0.25
    weighted_mix = mix_block * weight[:, None]
    summed = jnp.einsum("cs,kczl->kszl", weighted_mix, beam_gain * residual)
    return summed.astype(jnp.bfloat16)


def smooth_rows(padded, spacing, row_count):
    return (
        padded[0:row_count]
        + 2.0 * padded[spacing : spacing + row_count]
        + padded[2 * spacing : 2 * spacing + row_count]
    ) * 0.25


def smooth_cols(values, spacing):
    padded = jnp.pad(values, ((0, 0), (0, 0), (spacing, spacing)))
    return (
        padded[..., : -2 * spacing]
        + 2.0 * padded[..., spacing:-spacing]
        + padded[..., 2 * spacing :]
    ) * 0.25


def shrink(values, bound_value):
    return values - jnp.clip(values, -bound_value, bound_value)


def combine_scales(updated, smooth_one, coarse, fine_bound, coarse_bound):
    return (
        coarse
        + shrink(smooth_one - coarse, coarse_bound)
        + shrink(updated - smooth_one, fine_bound)
    )


def body(sky_data, beam_gains, mixing, noise_levels, threshold_levels, start_sources):
    strip_rows, source_count, col_count = start_sources.shape
    full_rows = strip_rows * lax.axis_size("chan")
    row_real, row_imag = dft_tables(full_rows)
    col_real, col_imag = dft_tables(col_count)
    col_cat = jnp.concatenate([col_real, col_imag], axis=1)
    col_back = jnp.concatenate([col_real, col_imag], axis=0)
    bounds = threshold_levels.astype(jnp.float32) * 0.05
    fine_bound = bounds[:, 0][:, None]
    coarse_bound = bounds[:, 1][:, None]
    first_row = lax.axis_index("chan") * strip_rows
    sources = start_sources
    for iteration in range(ITERS):
        rounded = sources.astype(jnp.bfloat16)
        gather = gather_all if iteration == 0 else gather_rows
        gathered = gather(rounded, "chan")
        by_source = jnp.transpose(gathered, (1, 0, 2))
        packed = jnp.dot(
            by_source.reshape(-1, col_count), col_cat, preferred_element_type=jnp.float32
        ).astype(jnp.bfloat16).reshape(source_count, full_rows, 2, col_count)
        real_prod = jnp.einsum("kr,srzl->kszl", row_real, packed, preferred_element_type=jnp.float32)
        imag_prod = jnp.einsum("kr,srzl->kszl", row_imag, packed, preferred_element_type=jnp.float32)
        fourier = jnp.stack(
            [real_prod[:, :, 0] - imag_prod[:, :, 1], real_prod[:, :, 1] + imag_prod[:, :, 0]],
            axis=2,
        )
        grad_local = block_gradient(fourier, sky_data, beam_gains, mixing, noise_levels)
        packed_grad = grad_local.reshape(full_rows, source_count * 2 * col_count)
        gradient = sum_rows(
            inverse_rows(row_real, row_imag, packed_grad, col_back, source_count, col_count),
            "chan",
        )
        updated = sources + gradient
        wide_pad = padded_2(updated, (("chan", 0),), 3)
        smooth_wide = smooth_cols(smooth_rows(wide_pad, 1, strip_rows + 4), 1)
        inside = (first_row - 2 + jnp.arange(strip_rows + 4) >= 0) & (
            first_row - 2 + jnp.arange(strip_rows + 4) < full_rows
        )
        smooth_wide = jnp.where(inside[:, None, None], smooth_wide, 0.0)
        smooth_one = smooth_wide[2 : 2 + strip_rows]
        coarse = smooth_cols(smooth_rows(smooth_wide, 2, strip_rows), 2)
        sources = combine_scales(updated, smooth_one, coarse, fine_bound, coarse_bound)
    return sources


def solution(mesh):
    return jax.shard_map(
        body,
        mesh=mesh,
        in_specs=(
            P("groups", "chan", None, None),
            P("groups", "chan", None),
            P(("groups", "chan"), None),
            P("chan"),
            P(),
            P(("groups", "chan"), None, None),
        ),
        out_specs=P(("groups", "chan"), None, None),
        check_vma=False,
    )
```

```python
import math

import jax
import jax.numpy as jnp
from jax import lax
from jax.sharding import PartitionSpec as P

ITERS = 2


def padded_2(cells, sides, width):
    for axis, dim in sides:
        count = lax.axis_size(axis)
        ends = count - 1
        head = lax.slice_in_dim(cells, 0, width, axis=dim)
        tail = lax.slice_in_dim(cells, cells.shape[dim] - width, cells.shape[dim], axis=dim)
        cells = jnp.concatenate(
            [
                lax.ppermute(tail, axis, [(i, (i + 1) % count) for i in range(ends)]),
                cells,
                lax.ppermute(head, axis, [((i + 1) % count, i) for i in range(ends)]),
            ],
            axis=dim,
        )
    return cells


def gather_all(strip, axis):
    count = lax.axis_size(axis)
    copies = jnp.broadcast_to(strip[None], (count,) + strip.shape)
    joined = lax.all_to_all(copies, axis, 0, 0, tiled=True)
    return joined.reshape((count * strip.shape[0],) + strip.shape[1:])


def gather_rows(strip, axis):
    count = lax.axis_size(axis)
    bits = count.bit_length() - 1
    assert 1 << bits == count
    own = lax.axis_index(axis)
    joined = strip
    for depth, bit in enumerate(reversed(range(bits))):
        partner = lax.ppermute(joined, axis, [(i, i ^ (1 << bit)) for i in range(count)])
        upper = ((own >> bit) & 1) == 1
        low = jnp.where(upper, partner, joined)
        high = jnp.where(upper, joined, partner)
        joined = jnp.stack([low, high], axis=depth)
    return joined.reshape((count * strip.shape[0],) + strip.shape[1:])


def sum_rows(values, axis):
    count = lax.axis_size(axis)
    half = count // 2
    parity = lax.axis_index(axis) % 2
    strip = values.shape[0] // count
    pairs = values.reshape((half, 2, strip) + values.shape[1:])
    even = pairs[:, 0]
    odd = pairs[:, 1]
    keep = jnp.where(parity == 1, odd, even)
    send = jnp.where(parity == 1, even, odd)
    moved = lax.ppermute(
        send.astype(jnp.bfloat16), axis, [(i, i ^ 1) for i in range(count)]
    )
    chip_sum = (keep + moved.astype(jnp.float32)).astype(jnp.bfloat16)
    groups = [list(range(p, count, 2)) for p in range(2)]
    received = lax.all_to_all(chip_sum, axis, 0, 0, tiled=True, axis_index_groups=groups)
    return received.astype(jnp.float32).sum(axis=0)


def dft_tables(length):
    positions = jnp.arange(length, dtype=jnp.int32)
    angles = (positions[:, None] * positions[None, :] % length).astype(jnp.float32) * (
        2.0 * math.pi / length
    )
    norm_factor = 1.0 / math.sqrt(length)
    return (
        (jnp.cos(angles) * norm_factor).astype(jnp.bfloat16),
        (-jnp.sin(angles) * norm_factor).astype(jnp.bfloat16),
    )


def column_part(rounded, col_cat):
    row_count, source_count, col_count = rounded.shape
    product = jnp.dot(
        rounded.reshape(row_count * source_count, col_count),
        col_cat,
        preferred_element_type=jnp.float32,
    )
    return product.astype(jnp.bfloat16).reshape(row_count, source_count * 2 * col_count)


def combine_forward(real_prod, imag_prod, source_count, col_count):
    real_prod = real_prod.reshape(real_prod.shape[0], source_count, 2, col_count)
    imag_prod = imag_prod.reshape(imag_prod.shape[0], source_count, 2, col_count)
    real_out = real_prod[:, :, 0] - imag_prod[:, :, 1]
    imag_out = real_prod[:, :, 1] + imag_prod[:, :, 0]
    return jnp.stack([real_out, imag_out], axis=2)


def inverse_rows(row_real, row_imag, packed_grad, col_back, source_count, col_count):
    real_prod = jnp.einsum("rk,kszl->rszl", row_real, packed_grad, preferred_element_type=jnp.float32)
    imag_prod = jnp.einsum("rk,kszl->rszl", row_imag, packed_grad, preferred_element_type=jnp.float32)
    real_out = real_prod[:, :, 0] + imag_prod[:, :, 1]
    imag_out = real_prod[:, :, 1] - imag_prod[:, :, 0]
    joined = jnp.concatenate([real_out, imag_out], axis=-1).astype(jnp.bfloat16)
    result = jnp.dot(
        joined.reshape(-1, 2 * col_count), col_back, preferred_element_type=jnp.float32
    )
    return result.reshape(real_prod.shape[0], source_count, col_count)


def block_gradient(fourier, data_block, beam_block, mix_block, level_block):
    predicted = jnp.einsum("ct,ktzl->kczl", mix_block, fourier)
    beam_gain = beam_block.astype(jnp.float32)[:, :, None, :]
    residual = data_block.astype(jnp.float32) - beam_gain * predicted
    weight = level_block.astype(jnp.float32) * 0.25
    weighted_mix = mix_block * weight[:, None]
    summed = jnp.einsum("cs,kczl->kszl", weighted_mix, beam_gain * residual)
    return summed.astype(jnp.bfloat16)


def smooth_rows(padded, spacing, row_count):
    return (
        padded[0:row_count]
        + 2.0 * padded[spacing : spacing + row_count]
        + padded[2 * spacing : 2 * spacing + row_count]
    ) * 0.25


def smooth_cols(values, spacing):
    padded = jnp.pad(values, ((0, 0), (0, 0), (spacing, spacing)))
    return (
        padded[..., : -2 * spacing]
        + 2.0 * padded[..., spacing:-spacing]
        + padded[..., 2 * spacing :]
    ) * 0.25


def shrink(values, bound_value):
    return values - jnp.clip(values, -bound_value, bound_value)


def combine_scales(updated, smooth_one, coarse, fine_bound, coarse_bound):
    return (
        coarse
        + shrink(smooth_one - coarse, coarse_bound)
        + shrink(updated - smooth_one, fine_bound)
    )


def body(sky_data, beam_gains, mixing, noise_levels, threshold_levels, start_sources):
    strip_rows, source_count, col_count = start_sources.shape
    full_rows = strip_rows * lax.axis_size("chan")
    row_real, row_imag = dft_tables(full_rows)
    col_real, col_imag = dft_tables(col_count)
    col_cat = jnp.concatenate([col_real, col_imag], axis=1)
    col_back = jnp.concatenate([col_real, col_imag], axis=0)
    bounds = threshold_levels.astype(jnp.float32) * 0.05
    fine_bound = bounds[:, 0][:, None]
    coarse_bound = bounds[:, 1][:, None]
    first_row = lax.axis_index("chan") * strip_rows
    sources = start_sources
    for iteration in range(ITERS):
        rounded = sources.astype(jnp.bfloat16)
        gather = gather_all if iteration == 0 else gather_rows
        gathered = gather(rounded, "chan")
        by_source = jnp.transpose(gathered, (1, 0, 2))
        packed = jnp.dot(
            by_source.reshape(-1, col_count), col_cat, preferred_element_type=jnp.float32
        ).astype(jnp.bfloat16).reshape(source_count, full_rows, 2, col_count)
        real_prod = jnp.einsum("kr,srzl->kszl", row_real, packed, preferred_element_type=jnp.float32)
        imag_prod = jnp.einsum("kr,srzl->kszl", row_imag, packed, preferred_element_type=jnp.float32)
        fourier = jnp.stack(
            [real_prod[:, :, 0] - imag_prod[:, :, 1], real_prod[:, :, 1] + imag_prod[:, :, 0]],
            axis=2,
        )
        grad_local = block_gradient(fourier, sky_data, beam_gains, mixing, noise_levels)
        packed_grad = grad_local
        gradient = sum_rows(
            inverse_rows(row_real, row_imag, packed_grad, col_back, source_count, col_count),
            "chan",
        )
        updated = sources + gradient
        wide_pad = padded_2(updated, (("chan", 0),), 3)
        smooth_wide = smooth_cols(smooth_rows(wide_pad, 1, strip_rows + 4), 1)
        inside = (first_row - 2 + jnp.arange(strip_rows + 4) >= 0) & (
            first_row - 2 + jnp.arange(strip_rows + 4) < full_rows
        )
        smooth_wide = jnp.where(inside[:, None, None], smooth_wide, 0.0)
        smooth_one = smooth_wide[2 : 2 + strip_rows]
        coarse = smooth_cols(smooth_rows(smooth_wide, 2, strip_rows), 2)
        sources = combine_scales(updated, smooth_one, coarse, fine_bound, coarse_bound)
    return sources


def solution(mesh):
    return jax.shard_map(
        body,
        mesh=mesh,
        in_specs=(
            P("groups", "chan", None, None),
            P("groups", "chan", None),
            P(("groups", "chan"), None),
            P("chan"),
            P(),
            P(("groups", "chan"), None, None),
        ),
        out_specs=P(("groups", "chan"), None, None),
        check_vma=False,
    )
```
